128 devices in a mesh: gx: 8 (over z, core), gy: 16 (over y, x).
Axes of the slice: x: 4, y: 4, z: 4, core: 2. Of those that a mesh axis runs over, the one named last changes fastest.
Arguments:
- records: bfloat16 [98304, 2048], P(('gx', 'gy')), may hold values from -4000 to 4000
- record_owner: int32 [98304], P(('gx', 'gy')), may hold values from 0 to 127, as said below
- record_field: int32 [98304], P(('gx', 'gy')), may hold values from 0 to 767, as said below
- filter_taps: float32 [2, 9], replicated, may hold values from 0.02 to 0.3
Outputs:
- modes: float32 [256, 3, 262144], P(None, None, ('gx', 'gy'))
- r_factor: float32 [256, 256], replicated
- first_factor: float32 [256, 256], replicated
The draws below stay inside these ranges and needn't reach their ends.
Inputs may be any that keep to these rules, and one draw needn't show every extreme that they name: `record_owner`: A device sends at most 12 records to any one owner; every device sends exactly 12 records to the owner whose index is its own plus 128 / 2, counted round; every owner is named by exactly 768 records over all devices. `record_field`: over all devices each pair of owner and field number occurs in exactly one record; field number 3 * s + c holds velocity component c of snapshot s.
All inputs are finite; a program needn't handle non-finite values.
Results may differ from the reference program's by a relative error of at most 0.0003.
Values may be sent and summed in bfloat16 or wider, within the bound.
No kernel may reach another device: no remote copies, remote signals or barrier semaphores. Data moves between devices by JAX's collectives and lax.ppermute only.
A program may use at most 128 MiB of HBM per device.

```python
import math
import jax
import jax.numpy as jnp
from jax import lax

SNAP = 256
PX = 16
PZ = 128
TAPS = 9
CELLS_DEV = 2048
REC_DEV = 768
RECORDS = 98304
N_GX = 8
N_GY = 16
DEVICES = 128


def plan_records(key):
    devices_all = DEVICES
    portion = REC_DEV // DEVICES
    half_way = devices_all // 2
    ordering = jax.random.permutation(jax.random.fold_in(key, 11), devices_all).astype(jnp.int32)
    lowest_at = jnp.argmin(ordering).astype(jnp.int32)
    held = ordering[half_way]
    ordering = ordering.at[lowest_at].set(held).at[half_way].set(0)
    weights = jnp.where(ordering < devices_all // 4, 2 * portion, jnp.where(ordering < 3 * (devices_all // 4), portion, 0)).astype(jnp.int32)
    begins = jnp.cumsum(weights) - weights
    finishes = begins + weights
    entries = jnp.arange(REC_DEV, dtype=jnp.int32)
    offsets = jnp.sum((finishes[None, :] <= entries[:, None]).astype(jnp.int32), axis=1)
    sources = jnp.arange(devices_all, dtype=jnp.int32)
    owners = (sources[:, None] + offsets[None, :]) % devices_all
    field_keys = jax.random.split(jax.random.fold_in(key, 12), devices_all)
    field_order = jax.vmap(lambda each_key: jax.random.permutation(each_key, REC_DEV))(field_keys).astype(jnp.int32)
    fields = field_order[owners, jnp.broadcast_to(entries[None, :], owners.shape)]
    slot_keys = jax.random.split(jax.random.fold_in(key, 13), devices_all)
    shuffle = jax.vmap(lambda each_key: jax.random.permutation(each_key, REC_DEV))(slot_keys).astype(jnp.int32)
    owners = jnp.take_along_axis(owners, shuffle, axis=1)
    fields = jnp.take_along_axis(fields, shuffle, axis=1)
    return (owners.reshape(-1).astype(jnp.int32), fields.reshape(-1).astype(jnp.int32))


def draw_record_owner(key, part):
    return plan_records(key)[0]


def draw_record_field(key, part):
    return plan_records(key)[1]


def draw_records(key, part):
    owners, fields = plan_records(key)
    snaps = fields // 3
    snap_scale = 10.0 ** jax.random.uniform(jax.random.fold_in(key, 21), (SNAP,), jnp.float32)
    cell_scale = 4.0 ** jax.random.uniform(jax.random.fold_in(key, 22), (DEVICES, CELLS_DEV), jnp.float32)
    level = owners.astype(jnp.float32) / (DEVICES - 1)
    owner_scale = 3.0 ** level
    base = jnp.clip(jax.random.normal(jax.random.fold_in(key, 25), (RECORDS, CELLS_DEV), jnp.float32), -4.0, 4.0)
    values = base * snap_scale[snaps][:, None] * owner_scale[:, None] * cell_scale[owners]
    return values.astype(jnp.bfloat16)


def setup_inputs(seed: int = 0) -> dict:
    seeds = jax.random.split(jax.random.key(seed), 5)
    records = draw_records(jax.random.fold_in(seeds[4], 71), 0)
    record_owner = draw_record_owner(jax.random.fold_in(seeds[4], 71), 0)
    record_field = draw_record_field(jax.random.fold_in(seeds[4], 71), 0)
    filter_taps = jnp.clip(jax.random.uniform(seeds[3], (2, TAPS), jnp.float32, 0.02, 0.3), 0.02, 0.3)
    return {"records": records, "record_owner": record_owner, "record_field": record_field, "filter_taps": filter_taps}


def circulant(tap_row, period):
    places = jnp.arange(period, dtype=jnp.int32)
    offsets = jnp.arange(9, dtype=jnp.int32) - 4
    target = (places[None, :, None] + offsets[:, None, None]) % period
    onehot = (target == places[None, None, :]).astype(jnp.float32)
    return jnp.einsum('k,kxa->xa', tap_row.astype(jnp.float32), onehot, precision=lax.Precision.HIGHEST)

def filter_fields(fields, stream_filter, span_filter):
    planes = fields.reshape(fields.shape[0], PX, PZ)
    planes = jnp.einsum('xa,faz->fxz', stream_filter, planes, precision=lax.Precision.HIGHEST)
    planes = jnp.einsum('fxb,zb->fxz', planes, span_filter, precision=lax.Precision.HIGHEST)
    return planes.reshape(fields.shape[0], PX * PZ)

def gram_of(matrix):
    return lax.dot_general(matrix.astype(jnp.float32), matrix.astype(jnp.float32), (((1,), (1,)), ((), ())), precision=lax.Precision.HIGHEST, preferred_element_type=jnp.float32)

def reference(records, record_owner, record_field, filter_taps):
    devices_all = N_GX * N_GY
    stream_filter = circulant(filter_taps[0], PX)
    span_filter = circulant(filter_taps[1], PZ)
    slot_table = jnp.zeros((devices_all * REC_DEV,), jnp.int32).at[record_owner * REC_DEV + record_field].set(jnp.arange(devices_all * REC_DEV, dtype=jnp.int32))
    slot_table = slot_table.reshape(devices_all, REC_DEV)

    def owner_fields(slot_row):
        fields = records[slot_row].astype(jnp.float32)
        fields = filter_fields(fields, stream_filter, span_filter)
        return fields.reshape(SNAP, 3 * CELLS_DEV)

    def first_term(slot_row):
        return owner_fields(slot_row)

    def accumulate_with(make):

        def accumulate(running, slot_row):
            return (running + gram_of(make(slot_row)), None)
        running, unused = lax.scan(accumulate, jnp.zeros((SNAP, SNAP), jnp.float32), slot_table)
        return running
    lower_one = jnp.linalg.cholesky(accumulate_with(first_term))

    def second_term(slot_row):
        return jax.scipy.linalg.solve_triangular(lower_one, owner_fields(slot_row), lower=True)
    lower_two = jnp.linalg.cholesky(accumulate_with(second_term))
    scale = math.sqrt(3.0 * CELLS_DEV * devices_all)

    def final_block(slot_row):
        return jax.scipy.linalg.solve_triangular(lower_two, second_term(slot_row), lower=True) * scale
    blocks = lax.map(final_block, slot_table)
    modes = blocks.reshape(devices_all, SNAP, 3, CELLS_DEV).transpose(1, 2, 0, 3).reshape(SNAP, 3, devices_all * CELLS_DEV)
    r_factor = jnp.dot(lower_two.T.astype(jnp.float32), lower_one.T.astype(jnp.float32), precision=lax.Precision.HIGHEST, preferred_element_type=jnp.float32) / scale
    first_factor = lower_one.T / scale
    return (modes, r_factor, first_factor)
```

```python
import math

import jax
import jax.numpy as jnp
from jax import lax
from jax.sharding import PartitionSpec as P

SNAP = 256
PX = 16
PZ = 128


def circulant(tap_row, period):
    places = jnp.arange(period, dtype=jnp.int32)
    offsets = jnp.arange(9, dtype=jnp.int32) - 4
    target = (places[None, :, None] + offsets[:, None, None]) % period
    onehot = (target == places[None, None, :]).astype(jnp.float32)
    return jnp.einsum("k,kxa->xa", tap_row, onehot, precision=lax.Precision.HIGHEST)


def filter_fields(fields, stream_filter, span_filter):
    planes = fields.reshape(fields.shape[0], PX, PZ)
    planes = jnp.einsum("xa,faz->fxz", stream_filter, planes, precision=lax.Precision.HIGHEST)
    planes = jnp.einsum("fxb,zb->fxz", planes, span_filter, precision=lax.Precision.HIGHEST)
    return planes.reshape(fields.shape[0], PX * PZ)


def gram_of(matrix):
    return lax.dot_general(
        matrix,
        matrix,
        (((1,), (1,)), ((), ())),
        precision=lax.Precision.HIGHEST,
        preferred_element_type=jnp.float32,
    )


def sum_over_devices(part, axes, devices_all):
    rows = part.reshape(devices_all, -1)
    rows = lax.all_to_all(rows, axes, 0, 0, tiled=True)
    total = jnp.sum(rows, axis=0, keepdims=True)
    total = jnp.broadcast_to(total, rows.shape)
    total = lax.all_to_all(total, axes, 0, 0, tiled=True)
    return total.reshape(part.shape)


def local(records, record_owner, record_field, filter_taps):
    devices_all = lax.axis_size(("gx", "gy"))
    rec_count = records.shape[0]
    cells = records.shape[1]
    capacity = 2 * (rec_count // devices_all)
    stream_filter = circulant(filter_taps[0], PX)
    span_filter = circulant(filter_taps[1], PZ)
    onehot = (record_owner[:, None] == jnp.arange(devices_all, dtype=jnp.int32)[None, :]).astype(
        jnp.int32
    )
    position = jnp.sum((jnp.cumsum(onehot, axis=0) - 1) * onehot, axis=1)
    buffer = (
        jnp.zeros((devices_all, capacity, cells), jnp.bfloat16)
        .at[record_owner, position]
        .set(records)
    )
    labels = (
        jnp.full((devices_all, capacity), -1, jnp.int32)
        .at[record_owner, position]
        .set(record_field)
    )
    arrived, arrived_labels = (
        lax.all_to_all(buffer, ("gx", "gy"), split_axis=0, concat_axis=0, tiled=True),
        lax.all_to_all(labels, ("gx", "gy"), split_axis=0, concat_axis=0, tiled=True),
    )
    flat_data = arrived.reshape(devices_all * capacity, cells)
    flat_labels = arrived_labels.reshape(devices_all * capacity)
    targets = jnp.where(flat_labels >= 0, flat_labels, rec_count)
    slot_table = (
        jnp.zeros((rec_count,), jnp.int32)
        .at[targets]
        .set(jnp.arange(devices_all * capacity, dtype=jnp.int32), mode="drop")
    )
    fields = flat_data[slot_table]
    fields = filter_fields(fields.astype(jnp.float32), stream_filter, span_filter)
    matrix = fields.reshape(SNAP, 3 * cells)
    lower_one = jnp.linalg.cholesky(sum_over_devices(gram_of(matrix), ("gx", "gy"), devices_all))
    basis_one = jax.scipy.linalg.solve_triangular(lower_one, matrix, lower=True)
    lower_two = jnp.linalg.cholesky(sum_over_devices(gram_of(basis_one), ("gx", "gy"), devices_all))
    scale = math.sqrt(3.0 * cells * devices_all)
    modes = jax.scipy.linalg.solve_triangular(lower_two, basis_one, lower=True) * scale
    r_factor = (
        jnp.dot(
            lower_two.T,
            lower_one.T,
            precision=lax.Precision.HIGHEST,
            preferred_element_type=jnp.float32,
        )
        / scale
    )
    first_factor = lower_one.T / scale
    return (modes.reshape(SNAP, 3, cells), r_factor, first_factor)


def solution(mesh):
    placed = (P(("gx", "gy"), None), P(("gx", "gy")), P(("gx", "gy")), P())
    return jax.shard_map(
        local,
        mesh=mesh,
        in_specs=placed,
        out_specs=(P(None, None, ("gx", "gy")), P(), P()),
        check_vma=False,
    )
```

```python
import math

import jax
import jax.numpy as jnp
from jax import lax
from jax.sharding import PartitionSpec as P

SNAP = 256
PX = 16
PZ = 128


def circulant(tap_row, period):
    places = jnp.arange(period, dtype=jnp.int32)
    offsets = jnp.arange(9, dtype=jnp.int32) - 4
    target = (places[None, :, None] + offsets[:, None, None]) % period
    onehot = (target == places[None, None, :]).astype(jnp.float32)
    return jnp.einsum("k,kxa->xa", tap_row, onehot, precision=lax.Precision.HIGHEST)


def filter_fields(fields, stream_filter, span_filter):
    planes = fields.reshape(fields.shape[0], PX, PZ)
    planes = jnp.einsum("xa,faz->fxz", stream_filter, planes, precision=lax.Precision.HIGHEST)
    planes = jnp.einsum("fxb,zb->fxz", planes, span_filter, precision=lax.Precision.HIGHEST)
    return planes.reshape(fields.shape[0], PX * PZ)


def gram_of(matrix):
    return lax.dot_general(
        matrix,
        matrix,
        (((1,), (1,)), ((), ())),
        precision=lax.Precision.HIGHEST,
        preferred_element_type=jnp.float32,
    )


def sum_over_devices(part, axes, devices_all):
    rows = part.reshape(devices_all, -1)
    rows = lax.all_to_all(rows, axes, 0, 0, tiled=True)
    total = jnp.sum(rows, axis=0, keepdims=True)
    total = jnp.broadcast_to(total, rows.shape)
    total = lax.all_to_all(total, axes, 0, 0, tiled=True)
    return total.reshape(part.shape)


def local(records, record_owner, record_field, filter_taps):
    devices_all = lax.axis_size(("gx", "gy"))
    rec_count = records.shape[0]
    cells = records.shape[1]
    capacity = 2 * (rec_count // devices_all)
    stream_filter = circulant(filter_taps[0], PX)
    span_filter = circulant(filter_taps[1], PZ)
    onehot = (record_owner[:, None] == jnp.arange(devices_all, dtype=jnp.int32)[None, :]).astype(
        jnp.int32
    )
    position = jnp.sum((jnp.cumsum(onehot, axis=0) - 1) * onehot, axis=1)
    slot = record_owner * capacity + position
    places = jnp.arange(devices_all * capacity, dtype=jnp.int32)
    pick = slot[None, :] == places[:, None]
    buffer = jnp.dot(
        pick.astype(jnp.bfloat16), records, preferred_element_type=jnp.float32
    ).astype(jnp.bfloat16)
    labels = jnp.sum(jnp.where(pick, record_field[None, :] + 1, 0), axis=1) - 1
    arrived, arrived_labels = (
        lax.all_to_all(
            buffer.reshape(devices_all, capacity, cells),
            ("gx", "gy"),
            split_axis=0,
            concat_axis=0,
            tiled=True,
        ),
        lax.all_to_all(
            labels.reshape(devices_all, capacity),
            ("gx", "gy"),
            split_axis=0,
            concat_axis=0,
            tiled=True,
        ),
    )
    flat_data = arrived.reshape(devices_all * capacity, cells)
    flat_labels = arrived_labels.reshape(devices_all * capacity)
    order = flat_labels[None, :] == jnp.arange(rec_count, dtype=jnp.int32)[:, None]
    fields = jnp.dot(order.astype(jnp.bfloat16), flat_data, preferred_element_type=jnp.float32)
    fields = filter_fields(fields, stream_filter, span_filter)
    matrix = fields.reshape(SNAP, 3 * cells)
    lower_one = jnp.linalg.cholesky(sum_over_devices(gram_of(matrix), ("gx", "gy"), devices_all))
    basis_one = jax.scipy.linalg.solve_triangular(lower_one, matrix, lower=True)
    lower_two = jnp.linalg.cholesky(sum_over_devices(gram_of(basis_one), ("gx", "gy"), devices_all))
    scale = math.sqrt(3.0 * cells * devices_all)
    modes = jax.scipy.linalg.solve_triangular(lower_two, basis_one, lower=True) * scale
    r_factor = (
        jnp.dot(
            lower_two.T,
            lower_one.T,
            precision=lax.Precision.HIGHEST,
            preferred_element_type=jnp.float32,
        )
        / scale
    )
    first_factor = lower_one.T / scale
    return (modes.reshape(SNAP, 3, cells), r_factor, first_factor)


def solution(mesh):
    placed = (P(("gx", "gy"), None), P(("gx", "gy")), P(("gx", "gy")), P())
    return jax.shard_map(
        local,
        mesh=mesh,
        in_specs=placed,
        out_specs=(P(None, None, ("gx", "gy")), P(), P()),
        check_vma=False,
    )
```

```python
import math

import jax
import jax.numpy as jnp
from jax import lax
from jax.sharding import PartitionSpec as P

SNAP = 256
PX = 16
PZ = 128


def circulant(tap_row, period):
    places = jnp.arange(period, dtype=jnp.int32)
    offsets = jnp.arange(9, dtype=jnp.int32) - 4
    target = (places[None, :, None] + offsets[:, None, None]) % period
    onehot = (target == places[None, None, :]).astype(jnp.float32)
    return jnp.einsum("k,kxa->xa", tap_row, onehot, precision=lax.Precision.HIGHEST)


def filter_fields(fields, stream_filter, span_filter):
    planes = fields.reshape(fields.shape[0], PX, PZ)
    planes = jnp.einsum("xa,faz->fxz", stream_filter, planes, precision=lax.Precision.HIGHEST)
    planes = jnp.einsum("fxb,zb->fxz", planes, span_filter, precision=lax.Precision.HIGHEST)
    return planes.reshape(fields.shape[0], PX * PZ)


def gram_of(matrix):
    return lax.dot_general(
        matrix,
        matrix,
        (((1,), (1,)), ((), ())),
        precision=lax.Precision.HIGHEST,
        preferred_element_type=jnp.float32,
    )


def sum_over_devices(part, axes, devices_all):
    rows = part.reshape(devices_all, -1)
    rows = lax.all_to_all(rows, axes, 0, 0, tiled=True)
    total = jnp.sum(rows, axis=0, keepdims=True)
    total = jnp.broadcast_to(total, rows.shape)
    total = lax.all_to_all(total, axes, 0, 0, tiled=True)
    return total.reshape(part.shape)


def local(records, record_owner, record_field, filter_taps):
    devices_all = lax.axis_size(("gx", "gy"))
    rec_count = records.shape[0]
    cells = records.shape[1]
    capacity = -(-2 * (rec_count // devices_all) // 16) * 16
    stream_filter = circulant(filter_taps[0], PX)
    span_filter = circulant(filter_taps[1], PZ)
    onehot = (record_owner[:, None] == jnp.arange(devices_all, dtype=jnp.int32)[None, :]).astype(
        jnp.int32
    )
    position = jnp.sum((jnp.cumsum(onehot, axis=0) - 1) * onehot, axis=1)
    slot = record_owner * capacity + position
    places = jnp.arange(devices_all * capacity, dtype=jnp.int32)
    pick = slot[None, :] == places[:, None]
    buffer = jnp.dot(
        pick.astype(jnp.bfloat16), records, preferred_element_type=jnp.float32
    ).astype(jnp.bfloat16)
    labels = jnp.sum(jnp.where(pick, record_field[None, :] + 1, 0), axis=1) - 1
    arrived, arrived_labels = (
        lax.all_to_all(
            buffer.reshape(devices_all, capacity, cells),
            ("gx", "gy"),
            split_axis=0,
            concat_axis=0,
            tiled=True,
        ),
        lax.all_to_all(
            labels.reshape(devices_all, capacity),
            ("gx", "gy"),
            split_axis=0,
            concat_axis=0,
            tiled=True,
        ),
    )
    flat_data = arrived.reshape(devices_all * capacity, cells)
    flat_labels = arrived_labels.reshape(devices_all * capacity)
    order = flat_labels[None, :] == jnp.arange(rec_count, dtype=jnp.int32)[:, None]
    fields = jnp.dot(order.astype(jnp.bfloat16), flat_data, preferred_element_type=jnp.float32)
    fields = filter_fields(fields, stream_filter, span_filter)
    matrix = fields.reshape(SNAP, 3 * cells)
    lower_one = jnp.linalg.cholesky(sum_over_devices(gram_of(matrix), ("gx", "gy"), devices_all))
    basis_one = jax.scipy.linalg.solve_triangular(lower_one, matrix, lower=True)
    lower_two = jnp.linalg.cholesky(sum_over_devices(gram_of(basis_one), ("gx", "gy"), devices_all))
    scale = math.sqrt(3.0 * cells * devices_all)
    modes = jax.scipy.linalg.solve_triangular(lower_two, basis_one, lower=True) * scale
    r_factor = (
        jnp.dot(
            lower_two.T,
            lower_one.T,
            precision=lax.Precision.HIGHEST,
            preferred_element_type=jnp.float32,
        )
        / scale
    )
    first_factor = lower_one.T / scale
    return (modes.reshape(SNAP, 3, cells), r_factor, first_factor)


def solution(mesh):
    placed = (P(("gx", "gy"), None), P(("gx", "gy")), P(("gx", "gy")), P())
    return jax.shard_map(
        local,
        mesh=mesh,
        in_specs=placed,
        out_specs=(P(None, None, ("gx", "gy")), P(), P()),
        check_vma=False,
    )
```

```python
import math

import jax
import jax.numpy as jnp
from jax import lax
from jax.sharding import PartitionSpec as P

SNAP = 256
PX = 16
PZ = 128


def circulant(tap_row, period):
    places = jnp.arange(period, dtype=jnp.int32)
    offsets = jnp.arange(9, dtype=jnp.int32) - 4
    target = (places[None, :, None] + offsets[:, None, None]) % period
    onehot = (target == places[None, None, :]).astype(jnp.float32)
    return jnp.einsum("k,kxa->xa", tap_row, onehot, precision=lax.Precision.HIGHEST)


def filter_fields(fields, stream_filter, span_filter):
    planes = fields.reshape(fields.shape[0], PX, PZ)
    planes = jnp.einsum("xa,faz->fxz", stream_filter, planes, precision=lax.Precision.HIGHEST)
    planes = jnp.einsum("fxb,zb->fxz", planes, span_filter, precision=lax.Precision.HIGHEST)
    return planes.reshape(fields.shape[0], PX * PZ)


def gram_of(matrix):
    return lax.dot_general(
        matrix,
        matrix,
        (((1,), (1,)), ((), ())),
        precision=lax.Precision.HIGHEST,
        preferred_element_type=jnp.float32,
    )


def high_dot(a, b, dims):
    return lax.dot_general(
        a, b, (dims, ((), ())), precision=lax.Precision.HIGHEST, preferred_element_type=jnp.float32
    )


def factor_and_inverse(gram):
    half = gram.shape[0] // 2
    gram = (gram + gram.T) / 2
    eye = jnp.eye(half, dtype=jnp.float32)
    lower_a = lax.linalg.cholesky(gram[:half, :half], symmetrize_input=False)
    inv_a = jnp.tril(lax.linalg.triangular_solve(lower_a, eye, left_side=True, lower=True))
    lower_b = high_dot(gram[half:, :half], inv_a, ((1,), (1,)))
    rest = gram[half:, half:] - high_dot(lower_b, lower_b, ((1,), (1,)))
    lower_c = lax.linalg.cholesky(rest, symmetrize_input=False)
    inv_c = jnp.tril(lax.linalg.triangular_solve(lower_c, eye, left_side=True, lower=True))
    inv_b = -high_dot(inv_c, high_dot(lower_b, inv_a, ((1,), (0,))), ((1,), (0,)))
    zero = jnp.zeros((half, half), jnp.float32)
    lower = jnp.block([[lower_a, zero], [lower_b, lower_c]])
    inverse = jnp.block([[inv_a, zero], [inv_b, inv_c]])
    return lower, inverse


def sum_over_devices(part, axes, devices_all):
    rows = part.reshape(devices_all, -1)
    rows = lax.all_to_all(rows, axes, 0, 0, tiled=True)
    total = jnp.sum(rows, axis=0, keepdims=True)
    total = jnp.broadcast_to(total, rows.shape)
    total = lax.all_to_all(total, axes, 0, 0, tiled=True)
    return total.reshape(part.shape)


def local(records, record_owner, record_field, filter_taps):
    devices_all = lax.axis_size(("gx", "gy"))
    rec_count = records.shape[0]
    cells = records.shape[1]
    capacity = -(-2 * (rec_count // devices_all) // 16) * 16
    stream_filter = circulant(filter_taps[0], PX)
    span_filter = circulant(filter_taps[1], PZ)
    onehot = (record_owner[:, None] == jnp.arange(devices_all, dtype=jnp.int32)[None, :]).astype(
        jnp.int32
    )
    position = jnp.sum((jnp.cumsum(onehot, axis=0) - 1) * onehot, axis=1)
    slot = record_owner * capacity + position
    places = jnp.arange(devices_all * capacity, dtype=jnp.int32)
    pick = slot[None, :] == places[:, None]
    buffer = jnp.dot(
        pick.astype(jnp.bfloat16), records, preferred_element_type=jnp.float32
    ).astype(jnp.bfloat16)
    labels = jnp.sum(jnp.where(pick, record_field[None, :] + 1, 0), axis=1) - 1
    arrived, arrived_labels = (
        lax.all_to_all(
            buffer.reshape(devices_all, capacity, cells),
            ("gx", "gy"),
            split_axis=0,
            concat_axis=0,
            tiled=True,
        ),
        lax.all_to_all(
            labels.reshape(devices_all, capacity),
            ("gx", "gy"),
            split_axis=0,
            concat_axis=0,
            tiled=True,
        ),
    )
    flat_data = arrived.reshape(devices_all * capacity, cells)
    flat_labels = arrived_labels.reshape(devices_all * capacity)
    target = (flat_labels % 3) * SNAP + flat_labels // 3
    target = jnp.where(flat_labels >= 0, target, -1)
    order = target[None, :] == jnp.arange(rec_count, dtype=jnp.int32)[:, None]
    fields = jnp.dot(order.astype(jnp.bfloat16), flat_data, preferred_element_type=jnp.float32)
    fields = filter_fields(fields, stream_filter, span_filter)
    matrix = fields.reshape(3, SNAP, cells)
    gram_one = high_dot(matrix, matrix, ((0, 2), (0, 2)))
    lower_one, inv_one = factor_and_inverse(sum_over_devices(gram_one, ("gx", "gy"), devices_all))
    basis_one = jnp.einsum("ij,cjk->cik", inv_one, matrix, precision=lax.Precision.HIGHEST)
    gram_two = high_dot(basis_one, basis_one, ((0, 2), (0, 2)))
    lower_two, inv_two = factor_and_inverse(sum_over_devices(gram_two, ("gx", "gy"), devices_all))
    scale = math.sqrt(3.0 * cells * devices_all)
    modes = jnp.einsum("ij,cjk->cik", inv_two, basis_one, precision=lax.Precision.HIGHEST) * scale
    r_factor = (
        jnp.dot(
            lower_two.T,
            lower_one.T,
            precision=lax.Precision.HIGHEST,
            preferred_element_type=jnp.float32,
        )
        / scale
    )
    first_factor = lower_one.T / scale
    return (modes.transpose(1, 0, 2), r_factor, first_factor)


def solution(mesh):
    placed = (P(("gx", "gy"), None), P(("gx", "gy")), P(("gx", "gy")), P())
    return jax.shard_map(
        local,
        mesh=mesh,
        in_specs=placed,
        out_specs=(P(None, None, ("gx", "gy")), P(), P()),
        check_vma=False,
    )
```

```python
import math

import jax
import jax.numpy as jnp
from jax import lax
from jax.sharding import PartitionSpec as P

SNAP = 256
PX = 16
PZ = 128


def circulant(tap_row, period):
    places = jnp.arange(period, dtype=jnp.int32)
    offsets = jnp.arange(9, dtype=jnp.int32) - 4
    target = (places[None, :, None] + offsets[:, None, None]) % period
    onehot = (target == places[None, None, :]).astype(jnp.float32)
    return jnp.einsum("k,kxa->xa", tap_row, onehot, precision=lax.Precision.HIGHEST)


def filter_fields(fields, stream_filter, span_filter):
    planes = fields.reshape(fields.shape[0], PX, PZ)
    planes = jnp.einsum("xa,faz->fxz", stream_filter, planes, precision=lax.Precision.HIGHEST)
    planes = jnp.einsum("fxb,zb->fxz", planes, span_filter, precision=lax.Precision.HIGHEST)
    return planes.reshape(fields.shape[0], PX * PZ)


def gram_of(matrix):
    return lax.dot_general(
        matrix,
        matrix,
        (((1,), (1,)), ((), ())),
        precision=lax.Precision.HIGHEST,
        preferred_element_type=jnp.float32,
    )


def high_dot(a, b, dims):
    return lax.dot_general(
        a, b, (dims, ((), ())), precision=lax.Precision.HIGHEST, preferred_element_type=jnp.float32
    )


def factor_and_inverse(gram):
    half = gram.shape[0] // 2
    gram = (gram + gram.T) / 2
    eye = jnp.eye(half, dtype=jnp.float32)
    lower_a = lax.linalg.cholesky(gram[:half, :half], symmetrize_input=False)
    inv_a = jnp.tril(lax.linalg.triangular_solve(lower_a, eye, left_side=True, lower=True))
    lower_b = high_dot(gram[half:, :half], inv_a, ((1,), (1,)))
    rest = gram[half:, half:] - high_dot(lower_b, lower_b, ((1,), (1,)))
    lower_c = lax.linalg.cholesky(rest, symmetrize_input=False)
    inv_c = jnp.tril(lax.linalg.triangular_solve(lower_c, eye, left_side=True, lower=True))
    inv_b = -high_dot(inv_c, high_dot(lower_b, inv_a, ((1,), (0,))), ((1,), (0,)))
    zero = jnp.zeros((half, half), jnp.float32)
    lower = jnp.block([[lower_a, zero], [lower_b, lower_c]])
    inverse = jnp.block([[inv_a, zero], [inv_b, inv_c]])
    return lower, inverse


def sum_over_devices(part, axes, devices_all):
    rows = part.reshape(devices_all, -1)
    rows = lax.all_to_all(rows, axes, 0, 0, tiled=True)
    total = jnp.sum(rows, axis=0, keepdims=True)
    total = jnp.broadcast_to(total, rows.shape)
    total = lax.all_to_all(total, axes, 0, 0, tiled=True)
    return total.reshape(part.shape)


def local(records, record_owner, record_field, filter_taps):
    devices_all = lax.axis_size(("gx", "gy"))
    rec_count = records.shape[0]
    cells = records.shape[1]
    capacity = 2 * (rec_count // devices_all)
    stream_filter = circulant(filter_taps[0], PX)
    span_filter = circulant(filter_taps[1], PZ)
    onehot = (record_owner[:, None] == jnp.arange(devices_all, dtype=jnp.int32)[None, :]).astype(
        jnp.int32
    )
    position = jnp.sum((jnp.cumsum(onehot, axis=0) - 1) * onehot, axis=1)
    slot = record_owner * capacity + position
    places = jnp.arange(devices_all * capacity, dtype=jnp.int32)
    pick = slot[None, :] == places[:, None]
    buffer = jnp.einsum(
        "kr,rab->kab",
        pick.astype(jnp.bfloat16),
        records.reshape(rec_count, PX, PZ),
        preferred_element_type=jnp.float32,
    ).astype(jnp.bfloat16)
    labels = jnp.sum(jnp.where(pick, record_field[None, :] + 1, 0), axis=1) - 1
    arrived, arrived_labels = (
        lax.all_to_all(
            buffer.reshape(devices_all, capacity, PX, PZ),
            ("gx", "gy"),
            split_axis=0,
            concat_axis=0,
            tiled=True,
        ),
        lax.all_to_all(
            labels.reshape(devices_all, capacity),
            ("gx", "gy"),
            split_axis=0,
            concat_axis=0,
            tiled=True,
        ),
    )
    flat_data = arrived.reshape(devices_all * capacity, PX, PZ)
    flat_labels = arrived_labels.reshape(devices_all * capacity)
    target = (flat_labels % 3) * SNAP + flat_labels // 3
    target = jnp.where(flat_labels >= 0, target, -1)
    order = target[None, :] == jnp.arange(rec_count, dtype=jnp.int32)[:, None]
    fields = jnp.einsum(
        "tk,kab->tab", order.astype(jnp.bfloat16), flat_data, preferred_element_type=jnp.float32
    ).reshape(rec_count, cells)
    fields = filter_fields(fields, stream_filter, span_filter)
    matrix = fields.reshape(3, SNAP, cells)
    gram_one = high_dot(matrix, matrix, ((0, 2), (0, 2)))
    lower_one, inv_one = factor_and_inverse(sum_over_devices(gram_one, ("gx", "gy"), devices_all))
    basis_one = jnp.einsum("ij,cjk->cik", inv_one, matrix, precision=lax.Precision.HIGHEST)
    gram_two = high_dot(basis_one, basis_one, ((0, 2), (0, 2)))
    lower_two, inv_two = factor_and_inverse(sum_over_devices(gram_two, ("gx", "gy"), devices_all))
    scale = math.sqrt(3.0 * cells * devices_all)
    modes = jnp.einsum("ij,cjk->cik", inv_two, basis_one, precision=lax.Precision.HIGHEST) * scale
    r_factor = (
        jnp.dot(
            lower_two.T,
            lower_one.T,
            precision=lax.Precision.HIGHEST,
            preferred_element_type=jnp.float32,
        )
        / scale
    )
    first_factor = lower_one.T / scale
    return (modes.transpose(1, 0, 2), r_factor, first_factor)


def solution(mesh):
    placed = (P(("gx", "gy"), None), P(("gx", "gy")), P(("gx", "gy")), P())
    return jax.shard_map(
        local,
        mesh=mesh,
        in_specs=placed,
        out_specs=(P(None, None, ("gx", "gy")), P(), P()),
        check_vma=False,
    )
```

```python
import math

import jax
import jax.numpy as jnp
from jax import lax
from jax.experimental import pallas as pl
from jax.experimental.pallas import tpu as pltpu
from jax.sharding import PartitionSpec as P

SNAP = 256
PX = 16
PZ = 128


def circulant(tap_row, period):
    places = jnp.arange(period, dtype=jnp.int32)
    offsets = jnp.arange(9, dtype=jnp.int32) - 4
    target = (places[None, :, None] + offsets[:, None, None]) % period
    onehot = (target == places[None, None, :]).astype(jnp.float32)
    return jnp.einsum("k,kxa->xa", tap_row, onehot, precision=lax.Precision.HIGHEST)


def split_three(matrix):
    high = lax.reduce_precision(matrix, exponent_bits=8, mantissa_bits=7)
    rest = matrix - high
    mid = lax.reduce_precision(rest, exponent_bits=8, mantissa_bits=7)
    low = rest - mid
    return jnp.concatenate([high, mid, low], axis=1).astype(jnp.bfloat16)


def filter_kernel(taps_ref, span_ref, planes_ref, out_ref, spread_ref):
    taps = taps_ref.shape[1]
    reach = (taps - 1) // 2
    span = span_ref[...]
    for x in range(PX):
        parts = jnp.dot(planes_ref[x], span, preferred_element_type=jnp.float32)
        spread_ref[x] = parts[:, :PZ] + parts[:, PZ : 2 * PZ] + parts[:, 2 * PZ :]
    for x in range(PX):
        acc = taps_ref[0, 0] * spread_ref[(x - reach) % PX]
        for k in range(1, taps):
            acc = acc + taps_ref[0, k] * spread_ref[(x + k - reach) % PX]
        out_ref[:, x * PZ : (x + 1) * PZ] = acc


def filter_planes(planes, filter_taps, rows=256):
    count = planes.shape[1]
    span = split_three(circulant(filter_taps[1], PZ).T)
    return pl.pallas_call(
        filter_kernel,
        grid=(count // rows,),
        in_specs=[
            pl.BlockSpec(memory_space=pltpu.SMEM),
            pl.BlockSpec((PZ, 3 * PZ), lambda i: (0, 0)),
            pl.BlockSpec((PX, rows, PZ), lambda i: (0, i, 0)),
        ],
        out_specs=pl.BlockSpec((rows, PX * PZ), lambda i: (i, 0)),
        out_shape=jax.ShapeDtypeStruct((count, PX * PZ), jnp.float32),
        scratch_shapes=[pltpu.VMEM((PX, rows, PZ), jnp.float32)],
    )(filter_taps, span, planes)


def gram_of(matrix):
    return lax.dot_general(
        matrix,
        matrix,
        (((1,), (1,)), ((), ())),
        precision=lax.Precision.HIGHEST,
        preferred_element_type=jnp.float32,
    )


def high_dot(a, b, dims):
    return lax.dot_general(
        a, b, (dims, ((), ())), precision=lax.Precision.HIGHEST, preferred_element_type=jnp.float32
    )


def factor_and_inverse(gram):
    half = gram.shape[0] // 2
    gram = (gram + gram.T) / 2
    eye = jnp.eye(half, dtype=jnp.float32)
    lower_a = lax.linalg.cholesky(gram[:half, :half], symmetrize_input=False)
    inv_a = jnp.tril(lax.linalg.triangular_solve(lower_a, eye, left_side=True, lower=True))
    lower_b = high_dot(gram[half:, :half], inv_a, ((1,), (1,)))
    rest = gram[half:, half:] - high_dot(lower_b, lower_b, ((1,), (1,)))
    lower_c = lax.linalg.cholesky(rest, symmetrize_input=False)
    inv_c = jnp.tril(lax.linalg.triangular_solve(lower_c, eye, left_side=True, lower=True))
    inv_b = -high_dot(inv_c, high_dot(lower_b, inv_a, ((1,), (0,))), ((1,), (0,)))
    zero = jnp.zeros((half, half), jnp.float32)
    lower = jnp.block([[lower_a, zero], [lower_b, lower_c]])
    inverse = jnp.block([[inv_a, zero], [inv_b, inv_c]])
    return lower, inverse


def sum_over_devices(part, axes, devices_all):
    rows = part.reshape(devices_all, -1)
    rows = lax.all_to_all(rows, axes, 0, 0, tiled=True)
    total = jnp.sum(rows, axis=0, keepdims=True)
    total = jnp.broadcast_to(total, rows.shape)
    total = lax.all_to_all(total, axes, 0, 0, tiled=True)
    return total.reshape(part.shape)


def local(records, record_owner, record_field, filter_taps):
    devices_all = lax.axis_size(("gx", "gy"))
    rec_count = records.shape[0]
    cells = records.shape[1]
    capacity = 2 * (rec_count // devices_all)
    onehot = (record_owner[:, None] == jnp.arange(devices_all, dtype=jnp.int32)[None, :]).astype(
        jnp.int32
    )
    position = jnp.sum((jnp.cumsum(onehot, axis=0) - 1) * onehot, axis=1)
    slot = record_owner * capacity + position
    places = jnp.arange(devices_all * capacity, dtype=jnp.int32)
    pick = slot[None, :] == places[:, None]
    buffer = jnp.einsum(
        "kr,rab->kab",
        pick.astype(jnp.bfloat16),
        records.reshape(rec_count, PX, PZ),
        preferred_element_type=jnp.float32,
    ).astype(jnp.bfloat16)
    labels = jnp.sum(jnp.where(pick, record_field[None, :] + 1, 0), axis=1) - 1
    arrived, arrived_labels = (
        lax.all_to_all(
            buffer.reshape(devices_all, capacity, PX, PZ),
            ("gx", "gy"),
            split_axis=0,
            concat_axis=0,
            tiled=True,
        ),
        lax.all_to_all(
            labels.reshape(devices_all, capacity),
            ("gx", "gy"),
            split_axis=0,
            concat_axis=0,
            tiled=True,
        ),
    )
    flat_data = arrived.reshape(devices_all * capacity, PX, PZ)
    flat_labels = arrived_labels.reshape(devices_all * capacity)
    target = (flat_labels % 3) * SNAP + flat_labels // 3
    target = jnp.where(flat_labels >= 0, target, -1)
    order = target[None, :] == jnp.arange(rec_count, dtype=jnp.int32)[:, None]
    planes = jnp.einsum(
        "tk,kab->atb", order.astype(jnp.bfloat16), flat_data, preferred_element_type=jnp.float32
    ).astype(jnp.bfloat16)
    fields = filter_planes(planes, filter_taps)
    matrix = fields.reshape(3, SNAP, cells)
    gram_one = high_dot(matrix, matrix, ((0, 2), (0, 2)))
    lower_one, inv_one = factor_and_inverse(sum_over_devices(gram_one, ("gx", "gy"), devices_all))
    basis_one = jnp.einsum("ij,cjk->cik", inv_one, matrix, precision=lax.Precision.HIGHEST)
    gram_two = high_dot(basis_one, basis_one, ((0, 2), (0, 2)))
    lower_two, inv_two = factor_and_inverse(sum_over_devices(gram_two, ("gx", "gy"), devices_all))
    scale = math.sqrt(3.0 * cells * devices_all)
    modes = jnp.einsum("ij,cjk->cik", inv_two, basis_one, precision=lax.Precision.HIGHEST) * scale
    r_factor = (
        jnp.dot(
            lower_two.T,
            lower_one.T,
            precision=lax.Precision.HIGHEST,
            preferred_element_type=jnp.float32,
        )
        / scale
    )
    first_factor = lower_one.T / scale
    return (modes.transpose(1, 0, 2), r_factor, first_factor)


def solution(mesh):
    placed = (P(("gx", "gy"), None), P(("gx", "gy")), P(("gx", "gy")), P())
    return jax.shard_map(
        local,
        mesh=mesh,
        in_specs=placed,
        out_specs=(P(None, None, ("gx", "gy")), P(), P()),
        check_vma=False,
    )
```

```python
import math

import jax
import jax.numpy as jnp
from jax import lax
from jax.experimental import pallas as pl
from jax.experimental.pallas import tpu as pltpu
from jax.sharding import PartitionSpec as P

SNAP = 256
PX = 16
PZ = 128


def circulant(tap_row, period):
    places = jnp.arange(period, dtype=jnp.int32)
    offsets = jnp.arange(9, dtype=jnp.int32) - 4
    target = (places[None, :, None] + offsets[:, None, None]) % period
    onehot = (target == places[None, None, :]).astype(jnp.float32)
    return jnp.einsum("k,kxa->xa", tap_row, onehot, precision=lax.Precision.HIGHEST)


def split_three(matrix):
    high = lax.reduce_precision(matrix, exponent_bits=8, mantissa_bits=7)
    rest = matrix - high
    mid = lax.reduce_precision(rest, exponent_bits=8, mantissa_bits=7)
    low = rest - mid
    return jnp.concatenate([high, mid, low], axis=1).astype(jnp.bfloat16)


def filter_kernel(taps_ref, span_ref, planes_ref, out_ref, gram_ref, spread_ref):
    taps = taps_ref.shape[1]
    reach = (taps - 1) // 2
    span = span_ref[...]

    @pl.when(pl.program_id(0) == 0)
    def _():
        gram_ref[...] = jnp.zeros(gram_ref.shape, jnp.float32)

    for x in range(PX):
        parts = jnp.dot(planes_ref[x], span, preferred_element_type=jnp.float32)
        spread_ref[x] = parts[:, :PZ] + parts[:, PZ : 2 * PZ] + parts[:, 2 * PZ :]
    for x in range(PX):
        acc = taps_ref[0, 0] * spread_ref[(x - reach) % PX]
        for k in range(1, taps):
            acc = acc + taps_ref[0, k] * spread_ref[(x + k - reach) % PX]
        out_ref[:, x * PZ : (x + 1) * PZ] = acc
    block = out_ref[...]
    gram_ref[...] += lax.dot_general(
        block,
        block,
        (((1,), (1,)), ((), ())),
        precision=lax.Precision.HIGHEST,
        preferred_element_type=jnp.float32,
    )


def filter_planes(planes, filter_taps):
    count = planes.shape[1]
    span = split_three(circulant(filter_taps[1], PZ).T)
    return pl.pallas_call(
        filter_kernel,
        grid=(count // SNAP,),
        in_specs=[
            pl.BlockSpec(memory_space=pltpu.SMEM),
            pl.BlockSpec((PZ, 3 * PZ), lambda i: (0, 0)),
            pl.BlockSpec((PX, SNAP, PZ), lambda i: (0, i, 0)),
        ],
        out_specs=[
            pl.BlockSpec((SNAP, PX * PZ), lambda i: (i, 0)),
            pl.BlockSpec((SNAP, SNAP), lambda i: (0, 0)),
        ],
        out_shape=[
            jax.ShapeDtypeStruct((count, PX * PZ), jnp.float32),
            jax.ShapeDtypeStruct((SNAP, SNAP), jnp.float32),
        ],
        scratch_shapes=[pltpu.VMEM((PX, SNAP, PZ), jnp.float32)],
    )(filter_taps, span, planes)


def gram_of(matrix):
    return lax.dot_general(
        matrix,
        matrix,
        (((1,), (1,)), ((), ())),
        precision=lax.Precision.HIGHEST,
        preferred_element_type=jnp.float32,
    )


def high_dot(a, b, dims):
    return lax.dot_general(
        a, b, (dims, ((), ())), precision=lax.Precision.HIGHEST, preferred_element_type=jnp.float32
    )


def factor_and_inverse(gram):
    half = gram.shape[0] // 2
    gram = (gram + gram.T) / 2
    eye = jnp.eye(half, dtype=jnp.float32)
    lower_a = lax.linalg.cholesky(gram[:half, :half], symmetrize_input=False)
    inv_a = jnp.tril(lax.linalg.triangular_solve(lower_a, eye, left_side=True, lower=True))
    lower_b = high_dot(gram[half:, :half], inv_a, ((1,), (1,)))
    rest = gram[half:, half:] - high_dot(lower_b, lower_b, ((1,), (1,)))
    lower_c = lax.linalg.cholesky(rest, symmetrize_input=False)
    inv_c = jnp.tril(lax.linalg.triangular_solve(lower_c, eye, left_side=True, lower=True))
    inv_b = -high_dot(inv_c, high_dot(lower_b, inv_a, ((1,), (0,))), ((1,), (0,)))
    zero = jnp.zeros((half, half), jnp.float32)
    lower = jnp.block([[lower_a, zero], [lower_b, lower_c]])
    inverse = jnp.block([[inv_a, zero], [inv_b, inv_c]])
    return lower, inverse


def sum_over_devices(part, axes, devices_all):
    rows = part.reshape(devices_all, -1)
    rows = lax.all_to_all(rows, axes, 0, 0, tiled=True)
    total = jnp.sum(rows, axis=0, keepdims=True)
    total = jnp.broadcast_to(total, rows.shape)
    total = lax.all_to_all(total, axes, 0, 0, tiled=True)
    return total.reshape(part.shape)


def local(records, record_owner, record_field, filter_taps):
    devices_all = lax.axis_size(("gx", "gy"))
    rec_count = records.shape[0]
    cells = records.shape[1]
    capacity = 2 * (rec_count // devices_all)
    onehot = (record_owner[:, None] == jnp.arange(devices_all, dtype=jnp.int32)[None, :]).astype(
        jnp.int32
    )
    position = jnp.sum((jnp.cumsum(onehot, axis=0) - 1) * onehot, axis=1)
    slot = record_owner * capacity + position
    places = jnp.arange(devices_all * capacity, dtype=jnp.int32)
    pick = slot[None, :] == places[:, None]
    buffer = jnp.einsum(
        "kr,rab->kab",
        pick.astype(jnp.bfloat16),
        records.reshape(rec_count, PX, PZ),
        preferred_element_type=jnp.float32,
    ).astype(jnp.bfloat16)
    labels = jnp.sum(jnp.where(pick, record_field[None, :] + 1, 0), axis=1) - 1
    arrived, arrived_labels = (
        lax.all_to_all(
            buffer.reshape(devices_all, capacity, PX, PZ),
            ("gx", "gy"),
            split_axis=0,
            concat_axis=0,
            tiled=True,
        ),
        lax.all_to_all(
            labels.reshape(devices_all, capacity),
            ("gx", "gy"),
            split_axis=0,
            concat_axis=0,
            tiled=True,
        ),
    )
    flat_data = arrived.reshape(devices_all * capacity, PX, PZ)
    flat_labels = arrived_labels.reshape(devices_all * capacity)
    target = (flat_labels % 3) * SNAP + flat_labels // 3
    target = jnp.where(flat_labels >= 0, target, -1)
    order = target[None, :] == jnp.arange(rec_count, dtype=jnp.int32)[:, None]
    planes = jnp.einsum(
        "tk,kab->atb", order.astype(jnp.bfloat16), flat_data, preferred_element_type=jnp.float32
    ).astype(jnp.bfloat16)
    fields, gram_one = filter_planes(planes, filter_taps)
    matrix = fields.reshape(3, SNAP, cells)
    lower_one, inv_one = factor_and_inverse(sum_over_devices(gram_one, ("gx", "gy"), devices_all))
    basis_one = jnp.einsum("ij,cjk->cik", inv_one, matrix, precision=lax.Precision.HIGHEST)
    gram_two = high_dot(basis_one, basis_one, ((0, 2), (0, 2)))
    lower_two, inv_two = factor_and_inverse(sum_over_devices(gram_two, ("gx", "gy"), devices_all))
    scale = math.sqrt(3.0 * cells * devices_all)
    modes = jnp.einsum("ij,cjk->cik", inv_two, basis_one, precision=lax.Precision.HIGHEST) * scale
    r_factor = (
        jnp.dot(
            lower_two.T,
            lower_one.T,
            precision=lax.Precision.HIGHEST,
            preferred_element_type=jnp.float32,
        )
        / scale
    )
    first_factor = lower_one.T / scale
    return (modes.transpose(1, 0, 2), r_factor, first_factor)


def solution(mesh):
    placed = (P(("gx", "gy"), None), P(("gx", "gy")), P(("gx", "gy")), P())
    return jax.shard_map(
        local,
        mesh=mesh,
        in_specs=placed,
        out_specs=(P(None, None, ("gx", "gy")), P(), P()),
        check_vma=False,
    )
```

```python
import functools
import math

import jax
import jax.numpy as jnp
from jax import lax
from jax.experimental import pallas as pl
from jax.experimental.pallas import tpu as pltpu
from jax.sharding import PartitionSpec as P

SNAP = 256
PX = 16
PZ = 128


def circulant(tap_row, period):
    places = jnp.arange(period, dtype=jnp.int32)
    offsets = jnp.arange(9, dtype=jnp.int32) - 4
    target = (places[None, :, None] + offsets[:, None, None]) % period
    onehot = (target == places[None, None, :]).astype(jnp.float32)
    return jnp.einsum("k,kxa->xa", tap_row, onehot, precision=lax.Precision.HIGHEST)


def split_three(matrix):
    high = lax.reduce_precision(matrix, exponent_bits=8, mantissa_bits=7)
    rest = matrix - high
    mid = lax.reduce_precision(rest, exponent_bits=8, mantissa_bits=7)
    low = rest - mid
    return jnp.concatenate([high, mid, low], axis=1).astype(jnp.bfloat16)


def filter_kernel(taps_ref, span_ref, planes_ref, out_ref, gram_ref, spread_ref):
    taps = taps_ref.shape[1]
    reach = (taps - 1) // 2
    span = span_ref[...]

    @pl.when(pl.program_id(0) == 0)
    def _():
        gram_ref[...] = jnp.zeros(gram_ref.shape, jnp.float32)

    for x in range(PX):
        parts = jnp.dot(planes_ref[x], span, preferred_element_type=jnp.float32)
        spread_ref[x] = parts[:, :PZ] + parts[:, PZ : 2 * PZ] + parts[:, 2 * PZ :]
    for x in range(PX):
        acc = taps_ref[0, 0] * spread_ref[(x - reach) % PX]
        for k in range(1, taps):
            acc = acc + taps_ref[0, k] * spread_ref[(x + k - reach) % PX]
        out_ref[:, x * PZ : (x + 1) * PZ] = acc
    block = out_ref[...]
    gram_ref[...] += lax.dot_general(
        block,
        block,
        (((1,), (1,)), ((), ())),
        precision=lax.Precision.HIGHEST,
        preferred_element_type=jnp.float32,
    )


def filter_planes(planes, filter_taps):
    count = planes.shape[1]
    span = split_three(circulant(filter_taps[1], PZ).T)
    return pl.pallas_call(
        filter_kernel,
        grid=(count // SNAP,),
        in_specs=[
            pl.BlockSpec(memory_space=pltpu.SMEM),
            pl.BlockSpec((PZ, 3 * PZ), lambda i: (0, 0)),
            pl.BlockSpec((PX, SNAP, PZ), lambda i: (0, i, 0)),
        ],
        out_specs=[
            pl.BlockSpec((SNAP, PX * PZ), lambda i: (i, 0)),
            pl.BlockSpec((SNAP, SNAP), lambda i: (0, 0)),
        ],
        out_shape=[
            jax.ShapeDtypeStruct((count, PX * PZ), jnp.float32),
            jax.ShapeDtypeStruct((SNAP, SNAP), jnp.float32),
        ],
        scratch_shapes=[pltpu.VMEM((PX, SNAP, PZ), jnp.float32)],
    )(filter_taps, span, planes)


def basis_kernel(inv_ref, matrix_ref, basis_ref, gram_ref):
    @pl.when(pl.program_id(0) == 0)
    def _():
        gram_ref[...] = jnp.zeros(gram_ref.shape, jnp.float32)

    basis = jnp.dot(
        inv_ref[...],
        matrix_ref[...],
        precision=lax.Precision.HIGHEST,
        preferred_element_type=jnp.float32,
    )
    basis_ref[...] = basis
    gram_ref[...] += lax.dot_general(
        basis,
        basis,
        (((1,), (1,)), ((), ())),
        precision=lax.Precision.HIGHEST,
        preferred_element_type=jnp.float32,
    )


def basis_and_gram(inverse, matrix):
    count, width = matrix.shape
    size = inverse.shape[0]
    return pl.pallas_call(
        basis_kernel,
        grid=(count // size,),
        in_specs=[
            pl.BlockSpec((size, size), lambda i: (0, 0)),
            pl.BlockSpec((size, width), lambda i: (i, 0)),
        ],
        out_specs=[
            pl.BlockSpec((size, width), lambda i: (i, 0)),
            pl.BlockSpec((size, size), lambda i: (0, 0)),
        ],
        out_shape=[
            jax.ShapeDtypeStruct((count, width), jnp.float32),
            jax.ShapeDtypeStruct((size, size), jnp.float32),
        ],
    )(inverse, matrix)


def modes_kernel(inv_ref, basis_ref, modes_ref, *, scale):
    modes_ref[...] = (
        jnp.dot(
            inv_ref[...],
            basis_ref[...],
            precision=lax.Precision.HIGHEST,
            preferred_element_type=jnp.float32,
        )
        * scale
    )


def modes_of(inverse, basis, scale):
    count, width = basis.shape
    size = inverse.shape[0]
    return pl.pallas_call(
        functools.partial(modes_kernel, scale=scale),
        grid=(count // size,),
        in_specs=[
            pl.BlockSpec((size, size), lambda i: (0, 0)),
            pl.BlockSpec((size, width), lambda i: (i, 0)),
        ],
        out_specs=pl.BlockSpec((size, width), lambda i: (i, 0)),
        out_shape=jax.ShapeDtypeStruct((count, width), jnp.float32),
    )(inverse, basis)


def gram_of(matrix):
    return lax.dot_general(
        matrix,
        matrix,
        (((1,), (1,)), ((), ())),
        precision=lax.Precision.HIGHEST,
        preferred_element_type=jnp.float32,
    )


def high_dot(a, b, dims):
    return lax.dot_general(
        a, b, (dims, ((), ())), precision=lax.Precision.HIGHEST, preferred_element_type=jnp.float32
    )


def factor_and_inverse(gram):
    half = gram.shape[0] // 2
    gram = (gram + gram.T) / 2
    eye = jnp.eye(half, dtype=jnp.float32)
    lower_a = lax.linalg.cholesky(gram[:half, :half], symmetrize_input=False)
    inv_a = jnp.tril(lax.linalg.triangular_solve(lower_a, eye, left_side=True, lower=True))
    lower_b = high_dot(gram[half:, :half], inv_a, ((1,), (1,)))
    rest = gram[half:, half:] - high_dot(lower_b, lower_b, ((1,), (1,)))
    lower_c = lax.linalg.cholesky(rest, symmetrize_input=False)
    inv_c = jnp.tril(lax.linalg.triangular_solve(lower_c, eye, left_side=True, lower=True))
    inv_b = -high_dot(inv_c, high_dot(lower_b, inv_a, ((1,), (0,))), ((1,), (0,)))
    zero = jnp.zeros((half, half), jnp.float32)
    lower = jnp.block([[lower_a, zero], [lower_b, lower_c]])
    inverse = jnp.block([[inv_a, zero], [inv_b, inv_c]])
    return lower, inverse


def sum_over_devices(part, axes, devices_all):
    rows = part.reshape(devices_all, -1)
    rows = lax.all_to_all(rows, axes, 0, 0, tiled=True)
    total = jnp.sum(rows, axis=0, keepdims=True)
    total = jnp.broadcast_to(total, rows.shape)
    total = lax.all_to_all(total, axes, 0, 0, tiled=True)
    return total.reshape(part.shape)


def local(records, record_owner, record_field, filter_taps):
    devices_all = lax.axis_size(("gx", "gy"))
    rec_count = records.shape[0]
    cells = records.shape[1]
    capacity = 2 * (rec_count // devices_all)
    onehot = (record_owner[:, None] == jnp.arange(devices_all, dtype=jnp.int32)[None, :]).astype(
        jnp.int32
    )
    position = jnp.sum((jnp.cumsum(onehot, axis=0) - 1) * onehot, axis=1)
    slot = record_owner * capacity + position
    places = jnp.arange(devices_all * capacity, dtype=jnp.int32)
    pick = slot[None, :] == places[:, None]
    buffer = jnp.einsum(
        "kr,rab->kab",
        pick.astype(jnp.bfloat16),
        records.reshape(rec_count, PX, PZ),
        preferred_element_type=jnp.float32,
    ).astype(jnp.bfloat16)
    labels = jnp.sum(jnp.where(pick, record_field[None, :] + 1, 0), axis=1) - 1
    arrived, arrived_labels = (
        lax.all_to_all(
            buffer.reshape(devices_all, capacity, PX, PZ),
            ("gx", "gy"),
            split_axis=0,
            concat_axis=0,
            tiled=True,
        ),
        lax.all_to_all(
            labels.reshape(devices_all, capacity),
            ("gx", "gy"),
            split_axis=0,
            concat_axis=0,
            tiled=True,
        ),
    )
    flat_data = arrived.reshape(devices_all * capacity, PX, PZ)
    flat_labels = arrived_labels.reshape(devices_all * capacity)
    target = (flat_labels % 3) * SNAP + flat_labels // 3
    target = jnp.where(flat_labels >= 0, target, -1)
    order = target[None, :] == jnp.arange(rec_count, dtype=jnp.int32)[:, None]
    planes = jnp.einsum(
        "tk,kab->atb", order.astype(jnp.bfloat16), flat_data, preferred_element_type=jnp.float32
    ).astype(jnp.bfloat16)
    fields, gram_one = filter_planes(planes, filter_taps)
    lower_one, inv_one = factor_and_inverse(sum_over_devices(gram_one, ("gx", "gy"), devices_all))
    basis_one, gram_two = basis_and_gram(inv_one, fields)
    lower_two, inv_two = factor_and_inverse(sum_over_devices(gram_two, ("gx", "gy"), devices_all))
    scale = math.sqrt(3.0 * cells * devices_all)
    modes = modes_of(inv_two, basis_one, scale).reshape(3, SNAP, cells)
    r_factor = (
        jnp.dot(
            lower_two.T,
            lower_one.T,
            precision=lax.Precision.HIGHEST,
            preferred_element_type=jnp.float32,
        )
        / scale
    )
    first_factor = lower_one.T / scale
    return (modes.transpose(1, 0, 2), r_factor, first_factor)


def solution(mesh):
    placed = (P(("gx", "gy"), None), P(("gx", "gy")), P(("gx", "gy")), P())
    return jax.shard_map(
        local,
        mesh=mesh,
        in_specs=placed,
        out_specs=(P(None, None, ("gx", "gy")), P(), P()),
        check_vma=False,
    )
```

```python
import functools
import math

import jax
import jax.numpy as jnp
from jax import lax
from jax.experimental import pallas as pl
from jax.experimental.pallas import tpu as pltpu
from jax.sharding import PartitionSpec as P

SNAP = 256
PX = 16
PZ = 128


def circulant(tap_row, period):
    places = jnp.arange(period, dtype=jnp.int32)
    offsets = jnp.arange(9, dtype=jnp.int32) - 4
    target = (places[None, :, None] + offsets[:, None, None]) % period
    onehot = (target == places[None, None, :]).astype(jnp.float32)
    return jnp.einsum("k,kxa->xa", tap_row, onehot, precision=lax.Precision.HIGHEST)


def split_three(matrix):
    high = lax.reduce_precision(matrix, exponent_bits=8, mantissa_bits=7)
    rest = matrix - high
    mid = lax.reduce_precision(rest, exponent_bits=8, mantissa_bits=7)
    low = rest - mid
    return jnp.concatenate([high, mid, low], axis=1).astype(jnp.bfloat16)


def filter_kernel(taps_ref, span_ref, planes_ref, out_ref, gram_ref, spread_ref):
    taps = taps_ref.shape[1]
    reach = (taps - 1) // 2
    span = span_ref[...]

    @pl.when(pl.program_id(0) == 0)
    def _():
        gram_ref[...] = jnp.zeros(gram_ref.shape, jnp.float32)

    for x in range(PX):
        parts = jnp.dot(planes_ref[x], span, preferred_element_type=jnp.float32)
        spread_ref[x] = parts[:, :PZ] + parts[:, PZ : 2 * PZ] + parts[:, 2 * PZ :]
    for x in range(PX):
        acc = taps_ref[0, 0] * spread_ref[(x - reach) % PX]
        for k in range(1, taps):
            acc = acc + taps_ref[0, k] * spread_ref[(x + k - reach) % PX]
        out_ref[:, x * PZ : (x + 1) * PZ] = acc
    block = out_ref[...]
    gram_ref[...] += lax.dot_general(
        block,
        block,
        (((1,), (1,)), ((), ())),
        precision=lax.Precision.HIGHEST,
        preferred_element_type=jnp.float32,
    )


def filter_planes(planes, filter_taps):
    count = planes.shape[1]
    span = split_three(circulant(filter_taps[1], PZ).T)
    return pl.pallas_call(
        filter_kernel,
        grid=(count // SNAP,),
        in_specs=[
            pl.BlockSpec(memory_space=pltpu.SMEM),
            pl.BlockSpec((PZ, 3 * PZ), lambda i: (0, 0)),
            pl.BlockSpec((PX, SNAP, PZ), lambda i: (0, i, 0)),
        ],
        out_specs=[
            pl.BlockSpec((SNAP, PX * PZ), lambda i: (i, 0)),
            pl.BlockSpec((SNAP, SNAP), lambda i: (0, 0)),
        ],
        out_shape=[
            jax.ShapeDtypeStruct((count, PX * PZ), jnp.float32),
            jax.ShapeDtypeStruct((SNAP, SNAP), jnp.float32),
        ],
        scratch_shapes=[pltpu.VMEM((PX, SNAP, PZ), jnp.float32)],
    )(filter_taps, span, planes)


def basis_kernel(inv_ref, matrix_ref, basis_ref, gram_ref):
    @pl.when(pl.program_id(0) == 0)
    def _():
        gram_ref[...] = jnp.zeros(gram_ref.shape, jnp.float32)

    basis = jnp.dot(
        inv_ref[...],
        matrix_ref[...],
        precision=lax.Precision.HIGHEST,
        preferred_element_type=jnp.float32,
    )
    basis_ref[...] = basis
    gram_ref[...] += lax.dot_general(
        basis,
        basis,
        (((1,), (1,)), ((), ())),
        precision=lax.Precision.HIGHEST,
        preferred_element_type=jnp.float32,
    )


def basis_and_gram(inverse, matrix):
    count, width = matrix.shape
    size = inverse.shape[0]
    return pl.pallas_call(
        basis_kernel,
        grid=(count // size,),
        in_specs=[
            pl.BlockSpec((size, size), lambda i: (0, 0)),
            pl.BlockSpec((size, width), lambda i: (i, 0)),
        ],
        out_specs=[
            pl.BlockSpec((size, width), lambda i: (i, 0)),
            pl.BlockSpec((size, size), lambda i: (0, 0)),
        ],
        out_shape=[
            jax.ShapeDtypeStruct((count, width), jnp.float32),
            jax.ShapeDtypeStruct((size, size), jnp.float32),
        ],
    )(inverse, matrix)


def modes_kernel(inv_ref, basis_ref, modes_ref, *, scale):
    modes_ref[...] = (
        jnp.dot(
            inv_ref[...],
            basis_ref[...],
            precision=lax.Precision.HIGHEST,
            preferred_element_type=jnp.float32,
        )
        * scale
    )


def modes_of(inverse, basis, scale):
    count, width = basis.shape
    size = inverse.shape[0]
    return pl.pallas_call(
        functools.partial(modes_kernel, scale=scale),
        grid=(count // size,),
        in_specs=[
            pl.BlockSpec((size, size), lambda i: (0, 0)),
            pl.BlockSpec((size, width), lambda i: (i, 0)),
        ],
        out_specs=pl.BlockSpec((size, width), lambda i: (i, 0)),
        out_shape=jax.ShapeDtypeStruct((count, width), jnp.float32),
    )(inverse, basis)


def swap_kernel(planes_ref, records_ref):
    records_ref[...] = pltpu.einshape("akb->kab", planes_ref[...])


def planes_to_records(planes, rows=256):
    width, count, lanes = planes.shape
    return pl.pallas_call(
        swap_kernel,
        grid=(count // rows,),
        in_specs=[pl.BlockSpec((width, rows, lanes), lambda i: (0, i, 0))],
        out_specs=pl.BlockSpec((rows, width, lanes), lambda i: (i, 0, 0)),
        out_shape=jax.ShapeDtypeStruct((count, width, lanes), planes.dtype),
    )(planes)


def gram_of(matrix):
    return lax.dot_general(
        matrix,
        matrix,
        (((1,), (1,)), ((), ())),
        precision=lax.Precision.HIGHEST,
        preferred_element_type=jnp.float32,
    )


def high_dot(a, b, dims):
    return lax.dot_general(
        a, b, (dims, ((), ())), precision=lax.Precision.HIGHEST, preferred_element_type=jnp.float32
    )


def factor_and_inverse(gram):
    half = gram.shape[0] // 2
    gram = (gram + gram.T) / 2
    eye = jnp.eye(half, dtype=jnp.float32)
    lower_a = lax.linalg.cholesky(gram[:half, :half], symmetrize_input=False)
    inv_a = jnp.tril(lax.linalg.triangular_solve(lower_a, eye, left_side=True, lower=True))
    lower_b = high_dot(gram[half:, :half], inv_a, ((1,), (1,)))
    rest = gram[half:, half:] - high_dot(lower_b, lower_b, ((1,), (1,)))
    lower_c = lax.linalg.cholesky(rest, symmetrize_input=False)
    inv_c = jnp.tril(lax.linalg.triangular_solve(lower_c, eye, left_side=True, lower=True))
    inv_b = -high_dot(inv_c, high_dot(lower_b, inv_a, ((1,), (0,))), ((1,), (0,)))
    zero = jnp.zeros((half, half), jnp.float32)
    lower = jnp.block([[lower_a, zero], [lower_b, lower_c]])
    inverse = jnp.block([[inv_a, zero], [inv_b, inv_c]])
    return lower, inverse


def sum_over_devices(part, axes, devices_all):
    rows = part.reshape(devices_all, -1)
    rows = lax.all_to_all(rows, axes, 0, 0, tiled=True)
    total = jnp.sum(rows, axis=0, keepdims=True)
    total = jnp.broadcast_to(total, rows.shape)
    total = lax.all_to_all(total, axes, 0, 0, tiled=True)
    return total.reshape(part.shape)


def local(records, record_owner, record_field, filter_taps):
    devices_all = lax.axis_size(("gx", "gy"))
    rec_count = records.shape[0]
    cells = records.shape[1]
    capacity = 2 * (rec_count // devices_all)
    onehot = (record_owner[:, None] == jnp.arange(devices_all, dtype=jnp.int32)[None, :]).astype(
        jnp.int32
    )
    position = jnp.sum((jnp.cumsum(onehot, axis=0) - 1) * onehot, axis=1)
    slot = record_owner * capacity + position
    places = jnp.arange(devices_all * capacity, dtype=jnp.int32)
    pick = slot[None, :] == places[:, None]
    buffer = jnp.einsum(
        "kr,rab->akb",
        pick.astype(jnp.bfloat16),
        records.reshape(rec_count, PX, PZ),
        preferred_element_type=jnp.float32,
    ).astype(jnp.bfloat16)
    buffer = planes_to_records(buffer)
    labels = jnp.sum(jnp.where(pick, record_field[None, :] + 1, 0), axis=1) - 1
    arrived, arrived_labels = (
        lax.all_to_all(
            buffer.reshape(devices_all, capacity, PX, PZ),
            ("gx", "gy"),
            split_axis=0,
            concat_axis=0,
            tiled=True,
        ),
        lax.all_to_all(
            labels.reshape(devices_all, capacity),
            ("gx", "gy"),
            split_axis=0,
            concat_axis=0,
            tiled=True,
        ),
    )
    flat_data = arrived.reshape(devices_all * capacity, PX, PZ)
    flat_labels = arrived_labels.reshape(devices_all * capacity)
    target = (flat_labels % 3) * SNAP + flat_labels // 3
    target = jnp.where(flat_labels >= 0, target, -1)
    order = target[None, :] == jnp.arange(rec_count, dtype=jnp.int32)[:, None]
    planes = jnp.einsum(
        "tk,kab->atb", order.astype(jnp.bfloat16), flat_data, preferred_element_type=jnp.float32
    ).astype(jnp.bfloat16)
    fields, gram_one = filter_planes(planes, filter_taps)
    lower_one, inv_one = factor_and_inverse(sum_over_devices(gram_one, ("gx", "gy"), devices_all))
    basis_one, gram_two = basis_and_gram(inv_one, fields)
    lower_two, inv_two = factor_and_inverse(sum_over_devices(gram_two, ("gx", "gy"), devices_all))
    scale = math.sqrt(3.0 * cells * devices_all)
    modes = modes_of(inv_two, basis_one, scale).reshape(3, SNAP, cells)
    r_factor = (
        jnp.dot(
            lower_two.T,
            lower_one.T,
            precision=lax.Precision.HIGHEST,
            preferred_element_type=jnp.float32,
        )
        / scale
    )
    first_factor = lower_one.T / scale
    return (modes.transpose(1, 0, 2), r_factor, first_factor)


def solution(mesh):
    placed = (P(("gx", "gy"), None), P(("gx", "gy")), P(("gx", "gy")), P())
    return jax.shard_map(
        local,
        mesh=mesh,
        in_specs=placed,
        out_specs=(P(None, None, ("gx", "gy")), P(), P()),
        check_vma=False,
    )
```

```python
import functools
import math

import jax
import jax.numpy as jnp
from jax import lax
from jax.experimental import pallas as pl
from jax.experimental.pallas import tpu as pltpu
from jax.sharding import PartitionSpec as P

SNAP = 256
PX = 16
PZ = 128


def circulant(tap_row, period):
    places = jnp.arange(period, dtype=jnp.int32)
    offsets = jnp.arange(9, dtype=jnp.int32) - 4
    target = (places[None, :, None] + offsets[:, None, None]) % period
    onehot = (target == places[None, None, :]).astype(jnp.float32)
    return jnp.einsum("k,kxa->xa", tap_row, onehot, precision=lax.Precision.HIGHEST)


def split_three(matrix):
    high = lax.reduce_precision(matrix, exponent_bits=8, mantissa_bits=7)
    rest = matrix - high
    mid = lax.reduce_precision(rest, exponent_bits=8, mantissa_bits=7)
    low = rest - mid
    return jnp.concatenate([high, mid, low], axis=1).astype(jnp.bfloat16)


def filter_kernel(taps_ref, span_ref, planes_ref, out_ref, gram_ref, spread_ref):
    taps = taps_ref.shape[1]
    reach = (taps - 1) // 2
    span = span_ref[...]

    @pl.when(pl.program_id(0) == 0)
    def _():
        gram_ref[...] = jnp.zeros(gram_ref.shape, jnp.float32)

    for x in range(PX):
        parts = jnp.dot(planes_ref[x], span, preferred_element_type=jnp.float32)
        spread_ref[x] = parts[:, :PZ] + parts[:, PZ : 2 * PZ] + parts[:, 2 * PZ :]
    for x in range(PX):
        acc = taps_ref[0, 0] * spread_ref[(x - reach) % PX]
        for k in range(1, taps):
            acc = acc + taps_ref[0, k] * spread_ref[(x + k - reach) % PX]
        out_ref[:, x * PZ : (x + 1) * PZ] = acc
    block = out_ref[...]
    gram_ref[...] += lax.dot_general(
        block,
        block,
        (((1,), (1,)), ((), ())),
        precision=lax.Precision.HIGHEST,
        preferred_element_type=jnp.float32,
    )


def filter_planes(planes, filter_taps):
    count = planes.shape[1]
    span = split_three(circulant(filter_taps[1], PZ).T)
    return pl.pallas_call(
        filter_kernel,
        grid=(count // SNAP,),
        in_specs=[
            pl.BlockSpec(memory_space=pltpu.SMEM),
            pl.BlockSpec((PZ, 3 * PZ), lambda i: (0, 0)),
            pl.BlockSpec((PX, SNAP, PZ), lambda i: (0, i, 0)),
        ],
        out_specs=[
            pl.BlockSpec((SNAP, PX * PZ), lambda i: (i, 0)),
            pl.BlockSpec((SNAP, SNAP), lambda i: (0, 0)),
        ],
        out_shape=[
            jax.ShapeDtypeStruct((count, PX * PZ), jnp.float32),
            jax.ShapeDtypeStruct((SNAP, SNAP), jnp.float32),
        ],
        scratch_shapes=[pltpu.VMEM((PX, SNAP, PZ), jnp.float32)],
    )(filter_taps, span, planes)


def basis_kernel(inv_ref, matrix_ref, basis_ref, gram_ref):
    @pl.when(pl.program_id(0) == 0)
    def _():
        gram_ref[...] = jnp.zeros(gram_ref.shape, jnp.float32)

    basis = jnp.dot(
        inv_ref[...],
        matrix_ref[...],
        precision=lax.Precision.HIGHEST,
        preferred_element_type=jnp.float32,
    )
    basis_ref[...] = basis
    gram_ref[...] += lax.dot_general(
        basis,
        basis,
        (((1,), (1,)), ((), ())),
        precision=lax.Precision.HIGHEST,
        preferred_element_type=jnp.float32,
    )


def basis_and_gram(inverse, matrix):
    count, width = matrix.shape
    size = inverse.shape[0]
    return pl.pallas_call(
        basis_kernel,
        grid=(count // size,),
        in_specs=[
            pl.BlockSpec((size, size), lambda i: (0, 0)),
            pl.BlockSpec((size, width), lambda i: (i, 0)),
        ],
        out_specs=[
            pl.BlockSpec((size, width), lambda i: (i, 0)),
            pl.BlockSpec((size, size), lambda i: (0, 0)),
        ],
        out_shape=[
            jax.ShapeDtypeStruct((count, width), jnp.float32),
            jax.ShapeDtypeStruct((size, size), jnp.float32),
        ],
    )(inverse, matrix)


def modes_kernel(inv_ref, basis_ref, modes_ref, *, scale):
    modes_ref[...] = (
        jnp.dot(
            inv_ref[...],
            basis_ref[...],
            precision=lax.Precision.HIGHEST,
            preferred_element_type=jnp.float32,
        )
        * scale
    )


def modes_of(inverse, basis, scale):
    count, width = basis.shape
    size = inverse.shape[0]
    return pl.pallas_call(
        functools.partial(modes_kernel, scale=scale),
        grid=(count // size,),
        in_specs=[
            pl.BlockSpec((size, size), lambda i: (0, 0)),
            pl.BlockSpec((size, width), lambda i: (i, 0)),
        ],
        out_specs=pl.BlockSpec((size, width), lambda i: (i, 0)),
        out_shape=jax.ShapeDtypeStruct((count, width), jnp.float32),
    )(inverse, basis)


def swap_kernel(planes_ref, records_ref):
    records_ref[...] = pltpu.einshape("akb->kab", planes_ref[...])


def planes_to_records(planes, rows=256):
    width, count, lanes = planes.shape
    return pl.pallas_call(
        swap_kernel,
        grid=(count // rows,),
        in_specs=[pl.BlockSpec((width, rows, lanes), lambda i: (0, i, 0))],
        out_specs=pl.BlockSpec((rows, width, lanes), lambda i: (i, 0, 0)),
        out_shape=jax.ShapeDtypeStruct((count, width, lanes), planes.dtype),
    )(planes)


def tri_inverse_kernel(lower_ref, inverse_ref):
    lower = lower_ref[...]
    size = lower.shape[0]
    row = lax.broadcasted_iota(jnp.int32, lower.shape, 0)
    col = lax.broadcasted_iota(jnp.int32, lower.shape, 1)
    inverse = jnp.where(row == col, 1.0 / lower, 0.0)
    level = 0
    while (1 << level) < size:
        same_pair = lax.shift_right_logical(row, level + 1) == lax.shift_right_logical(col, level + 1)
        other_half = lax.shift_right_logical(row, level) != lax.shift_right_logical(col, level)
        coupling = jnp.where(same_pair & other_half, lower, 0.0)
        step = jnp.dot(
            inverse, coupling, precision=lax.Precision.HIGHEST, preferred_element_type=jnp.float32
        )
        inverse = inverse - jnp.dot(
            step, inverse, precision=lax.Precision.HIGHEST, preferred_element_type=jnp.float32
        )
        level += 1
    inverse_ref[...] = inverse


def tri_inverse(lower):
    return pl.pallas_call(
        tri_inverse_kernel, out_shape=jax.ShapeDtypeStruct(lower.shape, jnp.float32)
    )(lower)


def gram_of(matrix):
    return lax.dot_general(
        matrix,
        matrix,
        (((1,), (1,)), ((), ())),
        precision=lax.Precision.HIGHEST,
        preferred_element_type=jnp.float32,
    )


def high_dot(a, b, dims):
    return lax.dot_general(
        a, b, (dims, ((), ())), precision=lax.Precision.HIGHEST, preferred_element_type=jnp.float32
    )


def factor_and_inverse(gram):
    half = gram.shape[0] // 2
    gram = (gram + gram.T) / 2
    lower_a = lax.linalg.cholesky(gram[:half, :half], symmetrize_input=False)
    inv_a = tri_inverse(lower_a)
    lower_b = high_dot(gram[half:, :half], inv_a, ((1,), (1,)))
    rest = gram[half:, half:] - high_dot(lower_b, lower_b, ((1,), (1,)))
    lower_c = lax.linalg.cholesky(rest, symmetrize_input=False)
    inv_c = tri_inverse(lower_c)
    inv_b = -high_dot(inv_c, high_dot(lower_b, inv_a, ((1,), (0,))), ((1,), (0,)))
    zero = jnp.zeros((half, half), jnp.float32)
    lower = jnp.block([[lower_a, zero], [lower_b, lower_c]])
    inverse = jnp.block([[inv_a, zero], [inv_b, inv_c]])
    return lower, inverse


def sum_over_devices(part, axes, devices_all):
    rows = part.reshape(devices_all, -1)
    rows = lax.all_to_all(rows, axes, 0, 0, tiled=True)
    total = jnp.sum(rows, axis=0, keepdims=True)
    total = jnp.broadcast_to(total, rows.shape)
    total = lax.all_to_all(total, axes, 0, 0, tiled=True)
    return total.reshape(part.shape)


def local(records, record_owner, record_field, filter_taps):
    devices_all = lax.axis_size(("gx", "gy"))
    rec_count = records.shape[0]
    cells = records.shape[1]
    capacity = 2 * (rec_count // devices_all)
    onehot = (record_owner[:, None] == jnp.arange(devices_all, dtype=jnp.int32)[None, :]).astype(
        jnp.int32
    )
    position = jnp.sum((jnp.cumsum(onehot, axis=0) - 1) * onehot, axis=1)
    slot = record_owner * capacity + position
    places = jnp.arange(devices_all * capacity, dtype=jnp.int32)
    pick = slot[None, :] == places[:, None]
    buffer = jnp.einsum(
        "kr,rab->akb",
        pick.astype(jnp.bfloat16),
        records.reshape(rec_count, PX, PZ),
        preferred_element_type=jnp.float32,
    ).astype(jnp.bfloat16)
    buffer = planes_to_records(buffer)
    labels = jnp.sum(jnp.where(pick, record_field[None, :] + 1, 0), axis=1) - 1
    arrived, arrived_labels = (
        lax.all_to_all(
            buffer.reshape(devices_all, capacity, PX, PZ),
            ("gx", "gy"),
            split_axis=0,
            concat_axis=0,
            tiled=True,
        ),
        lax.all_to_all(
            labels.reshape(devices_all, capacity),
            ("gx", "gy"),
            split_axis=0,
            concat_axis=0,
            tiled=True,
        ),
    )
    flat_data = arrived.reshape(devices_all * capacity, PX, PZ)
    flat_labels = arrived_labels.reshape(devices_all * capacity)
    target = (flat_labels % 3) * SNAP + flat_labels // 3
    target = jnp.where(flat_labels >= 0, target, -1)
    order = target[None, :] == jnp.arange(rec_count, dtype=jnp.int32)[:, None]
    planes = jnp.einsum(
        "tk,kab->atb", order.astype(jnp.bfloat16), flat_data, preferred_element_type=jnp.float32
    ).astype(jnp.bfloat16)
    fields, gram_one = filter_planes(planes, filter_taps)
    lower_one, inv_one = factor_and_inverse(sum_over_devices(gram_one, ("gx", "gy"), devices_all))
    basis_one, gram_two = basis_and_gram(inv_one, fields)
    lower_two, inv_two = factor_and_inverse(sum_over_devices(gram_two, ("gx", "gy"), devices_all))
    scale = math.sqrt(3.0 * cells * devices_all)
    modes = modes_of(inv_two, basis_one, scale).reshape(3, SNAP, cells)
    r_factor = (
        jnp.dot(
            lower_two.T,
            lower_one.T,
            precision=lax.Precision.HIGHEST,
            preferred_element_type=jnp.float32,
        )
        / scale
    )
    first_factor = lower_one.T / scale
    return (modes.transpose(1, 0, 2), r_factor, first_factor)


def solution(mesh):
    placed = (P(("gx", "gy"), None), P(("gx", "gy")), P(("gx", "gy")), P())
    return jax.shard_map(
        local,
        mesh=mesh,
        in_specs=placed,
        out_specs=(P(None, None, ("gx", "gy")), P(), P()),
        check_vma=False,
    )
```

```python
import functools
import math

import jax
import jax.numpy as jnp
from jax import lax
from jax.experimental import pallas as pl
from jax.experimental.pallas import tpu as pltpu
from jax.sharding import PartitionSpec as P

SNAP = 256
PX = 16
PZ = 128


def circulant(tap_row, period):
    places = jnp.arange(period, dtype=jnp.int32)
    offsets = jnp.arange(9, dtype=jnp.int32) - 4
    target = (places[None, :, None] + offsets[:, None, None]) % period
    onehot = (target == places[None, None, :]).astype(jnp.float32)
    return jnp.einsum("k,kxa->xa", tap_row, onehot, precision=lax.Precision.HIGHEST)


def split_three(matrix):
    high = lax.reduce_precision(matrix, exponent_bits=8, mantissa_bits=7)
    rest = matrix - high
    mid = lax.reduce_precision(rest, exponent_bits=8, mantissa_bits=7)
    low = rest - mid
    return jnp.concatenate([high, mid, low], axis=1).astype(jnp.bfloat16)


def filter_kernel(taps_ref, span_ref, planes_ref, out_ref, gram_ref, spread_ref):
    taps = taps_ref.shape[1]
    reach = (taps - 1) // 2
    span = span_ref[...]

    @pl.when(pl.program_id(0) == 0)
    def _():
        gram_ref[...] = jnp.zeros(gram_ref.shape, jnp.float32)

    for x in range(PX):
        parts = jnp.dot(planes_ref[x], span, preferred_element_type=jnp.float32)
        spread_ref[x] = parts[:, :PZ] + parts[:, PZ : 2 * PZ] + parts[:, 2 * PZ :]
    for x in range(PX):
        acc = taps_ref[0, 0] * spread_ref[(x - reach) % PX]
        for k in range(1, taps):
            acc = acc + taps_ref[0, k] * spread_ref[(x + k - reach) % PX]
        out_ref[:, x * PZ : (x + 1) * PZ] = acc
    block = out_ref[...]
    gram_ref[...] += lax.dot_general(
        block,
        block,
        (((1,), (1,)), ((), ())),
        precision=lax.Precision.HIGHEST,
        preferred_element_type=jnp.float32,
    )


def filter_planes(planes, filter_taps):
    count = planes.shape[1]
    span = split_three(circulant(filter_taps[1], PZ).T)
    return pl.pallas_call(
        filter_kernel,
        grid=(count // SNAP,),
        in_specs=[
            pl.BlockSpec(memory_space=pltpu.SMEM),
            pl.BlockSpec((PZ, 3 * PZ), lambda i: (0, 0)),
            pl.BlockSpec((PX, SNAP, PZ), lambda i: (0, i, 0)),
        ],
        out_specs=[
            pl.BlockSpec((SNAP, PX * PZ), lambda i: (i, 0)),
            pl.BlockSpec((SNAP, SNAP), lambda i: (0, 0)),
        ],
        out_shape=[
            jax.ShapeDtypeStruct((count, PX * PZ), jnp.float32),
            jax.ShapeDtypeStruct((SNAP, SNAP), jnp.float32),
        ],
        scratch_shapes=[pltpu.VMEM((PX, SNAP, PZ), jnp.float32)],
    )(filter_taps, span, planes)


def basis_kernel(inv_ref, matrix_ref, basis_ref, gram_ref):
    @pl.when(pl.program_id(0) == 0)
    def _():
        gram_ref[...] = jnp.zeros(gram_ref.shape, jnp.float32)

    basis = jnp.dot(
        inv_ref[...],
        matrix_ref[...],
        precision=lax.Precision.HIGHEST,
        preferred_element_type=jnp.float32,
    )
    basis_ref[...] = basis
    gram_ref[...] += lax.dot_general(
        basis,
        basis,
        (((1,), (1,)), ((), ())),
        precision=lax.Precision.HIGHEST,
        preferred_element_type=jnp.float32,
    )


def basis_and_gram(inverse, matrix):
    count, width = matrix.shape
    size = inverse.shape[0]
    return pl.pallas_call(
        basis_kernel,
        grid=(count // size,),
        in_specs=[
            pl.BlockSpec((size, size), lambda i: (0, 0)),
            pl.BlockSpec((size, width), lambda i: (i, 0)),
        ],
        out_specs=[
            pl.BlockSpec((size, width), lambda i: (i, 0)),
            pl.BlockSpec((size, size), lambda i: (0, 0)),
        ],
        out_shape=[
            jax.ShapeDtypeStruct((count, width), jnp.float32),
            jax.ShapeDtypeStruct((size, size), jnp.float32),
        ],
    )(inverse, matrix)


def modes_kernel(inv_ref, basis_ref, modes_ref, *, scale):
    modes_ref[...] = (
        jnp.dot(
            inv_ref[...],
            basis_ref[...],
            precision=lax.Precision.HIGHEST,
            preferred_element_type=jnp.float32,
        )
        * scale
    )


def modes_of(inverse, basis, scale):
    count, width = basis.shape
    size = inverse.shape[0]
    return pl.pallas_call(
        functools.partial(modes_kernel, scale=scale),
        grid=(count // size,),
        in_specs=[
            pl.BlockSpec((size, size), lambda i: (0, 0)),
            pl.BlockSpec((size, width), lambda i: (i, 0)),
        ],
        out_specs=pl.BlockSpec((size, width), lambda i: (i, 0)),
        out_shape=jax.ShapeDtypeStruct((count, width), jnp.float32),
    )(inverse, basis)


def swap_kernel(planes_ref, records_ref):
    records_ref[...] = pltpu.einshape("akb->kab", planes_ref[...])


def planes_to_records(planes, rows=256):
    width, count, lanes = planes.shape
    return pl.pallas_call(
        swap_kernel,
        grid=(count // rows,),
        in_specs=[pl.BlockSpec((width, rows, lanes), lambda i: (0, i, 0))],
        out_specs=pl.BlockSpec((rows, width, lanes), lambda i: (i, 0, 0)),
        out_shape=jax.ShapeDtypeStruct((count, width, lanes), planes.dtype),
    )(planes)


def doubling_inverse(lower):
    size = lower.shape[0]
    row = lax.broadcasted_iota(jnp.int32, lower.shape, 0)
    col = lax.broadcasted_iota(jnp.int32, lower.shape, 1)
    inverse = jnp.where(row == col, 1.0 / lower, 0.0)
    level = 0
    while (1 << level) < size:
        same_pair = lax.shift_right_logical(row, level + 1) == lax.shift_right_logical(col, level + 1)
        other_half = lax.shift_right_logical(row, level) != lax.shift_right_logical(col, level)
        coupling = jnp.where(same_pair & other_half, lower, 0.0)
        step = jnp.dot(
            inverse, coupling, precision=lax.Precision.HIGHEST, preferred_element_type=jnp.float32
        )
        inverse = inverse - jnp.dot(
            step, inverse, precision=lax.Precision.HIGHEST, preferred_element_type=jnp.float32
        )
        level += 1
    return inverse


def nt_dot(a, b):
    return lax.dot_general(
        a, b, (((1,), (1,)), ((), ())), precision=lax.Precision.HIGHEST,
        preferred_element_type=jnp.float32,
    )


def nn_dot(a, b):
    return jnp.dot(a, b, precision=lax.Precision.HIGHEST, preferred_element_type=jnp.float32)


def first_half_kernel(lower_a_ref, gram_ref, inv_a_ref, lower_b_ref, rest_ref):
    half = lower_a_ref.shape[0]
    inv_a = doubling_inverse(lower_a_ref[...])
    inv_a_ref[...] = inv_a
    lower_b = nt_dot(gram_ref[half:, :half], inv_a)
    lower_b_ref[...] = lower_b
    rest_ref[...] = gram_ref[half:, half:] - nt_dot(lower_b, lower_b)


def second_half_kernel(lower_a_ref, lower_b_ref, lower_c_ref, inv_a_ref, lower_ref, inverse_ref):
    half = lower_a_ref.shape[0]
    inv_c = doubling_inverse(lower_c_ref[...])
    inv_a = inv_a_ref[...]
    zero = jnp.zeros((half, half), jnp.float32)
    lower_ref[:half, :half] = lower_a_ref[...]
    lower_ref[:half, half:] = zero
    lower_ref[half:, :half] = lower_b_ref[...]
    lower_ref[half:, half:] = lower_c_ref[...]
    inverse_ref[:half, :half] = inv_a
    inverse_ref[:half, half:] = zero
    inverse_ref[half:, :half] = -nn_dot(inv_c, nn_dot(lower_b_ref[...], inv_a))
    inverse_ref[half:, half:] = inv_c


def gram_of(matrix):
    return lax.dot_general(
        matrix,
        matrix,
        (((1,), (1,)), ((), ())),
        precision=lax.Precision.HIGHEST,
        preferred_element_type=jnp.float32,
    )


def high_dot(a, b, dims):
    return lax.dot_general(
        a, b, (dims, ((), ())), precision=lax.Precision.HIGHEST, preferred_element_type=jnp.float32
    )


def factor_and_inverse(gram):
    size = gram.shape[0]
    half = size // 2
    gram = (gram + gram.T) / 2
    lower_a = lax.linalg.cholesky(gram[:half, :half], symmetrize_input=False)
    square = jax.ShapeDtypeStruct((half, half), jnp.float32)
    inv_a, lower_b, rest = pl.pallas_call(
        first_half_kernel, out_shape=[square, square, square]
    )(lower_a, gram)
    lower_c = lax.linalg.cholesky(rest, symmetrize_input=False)
    full = jax.ShapeDtypeStruct((size, size), jnp.float32)
    lower, inverse = pl.pallas_call(
        second_half_kernel, out_shape=[full, full]
    )(lower_a, lower_b, lower_c, inv_a)
    return lower, inverse


def sum_over_devices(part, axes, devices_all):
    rows = part.reshape(devices_all, -1)
    rows = lax.all_to_all(rows, axes, 0, 0, tiled=True)
    total = jnp.sum(rows, axis=0, keepdims=True)
    total = jnp.broadcast_to(total, rows.shape)
    total = lax.all_to_all(total, axes, 0, 0, tiled=True)
    return total.reshape(part.shape)


def local(records, record_owner, record_field, filter_taps):
    devices_all = lax.axis_size(("gx", "gy"))
    rec_count = records.shape[0]
    cells = records.shape[1]
    capacity = 2 * (rec_count // devices_all)
    onehot = (record_owner[:, None] == jnp.arange(devices_all, dtype=jnp.int32)[None, :]).astype(
        jnp.int32
    )
    position = jnp.sum((jnp.cumsum(onehot, axis=0) - 1) * onehot, axis=1)
    slot = record_owner * capacity + position
    places = jnp.arange(devices_all * capacity, dtype=jnp.int32)
    pick = slot[None, :] == places[:, None]
    buffer = jnp.einsum(
        "kr,rab->akb",
        pick.astype(jnp.bfloat16),
        records.reshape(rec_count, PX, PZ),
        preferred_element_type=jnp.float32,
    ).astype(jnp.bfloat16)
    buffer = planes_to_records(buffer)
    labels = jnp.sum(jnp.where(pick, record_field[None, :] + 1, 0), axis=1) - 1
    arrived, arrived_labels = (
        lax.all_to_all(
            buffer.reshape(devices_all, capacity, PX, PZ),
            ("gx", "gy"),
            split_axis=0,
            concat_axis=0,
            tiled=True,
        ),
        lax.all_to_all(
            labels.reshape(devices_all, capacity),
            ("gx", "gy"),
            split_axis=0,
            concat_axis=0,
            tiled=True,
        ),
    )
    flat_data = arrived.reshape(devices_all * capacity, PX, PZ)
    flat_labels = arrived_labels.reshape(devices_all * capacity)
    target = (flat_labels % 3) * SNAP + flat_labels // 3
    target = jnp.where(flat_labels >= 0, target, -1)
    order = target[None, :] == jnp.arange(rec_count, dtype=jnp.int32)[:, None]
    planes = jnp.einsum(
        "tk,kab->atb", order.astype(jnp.bfloat16), flat_data, preferred_element_type=jnp.float32
    ).astype(jnp.bfloat16)
    fields, gram_one = filter_planes(planes, filter_taps)
    lower_one, inv_one = factor_and_inverse(sum_over_devices(gram_one, ("gx", "gy"), devices_all))
    basis_one, gram_two = basis_and_gram(inv_one, fields)
    lower_two, inv_two = factor_and_inverse(sum_over_devices(gram_two, ("gx", "gy"), devices_all))
    scale = math.sqrt(3.0 * cells * devices_all)
    modes = modes_of(inv_two, basis_one, scale).reshape(3, SNAP, cells)
    r_factor = (
        jnp.dot(
            lower_two.T,
            lower_one.T,
            precision=lax.Precision.HIGHEST,
            preferred_element_type=jnp.float32,
        )
        / scale
    )
    first_factor = lower_one.T / scale
    return (modes.transpose(1, 0, 2), r_factor, first_factor)


def solution(mesh):
    placed = (P(("gx", "gy"), None), P(("gx", "gy")), P(("gx", "gy")), P())
    return jax.shard_map(
        local,
        mesh=mesh,
        in_specs=placed,
        out_specs=(P(None, None, ("gx", "gy")), P(), P()),
        check_vma=False,
    )
```

```python
import functools
import math

import jax
import jax.numpy as jnp
from jax import lax
from jax.experimental import pallas as pl
from jax.experimental.pallas import tpu as pltpu
from jax.sharding import PartitionSpec as P

SNAP = 256
PX = 16
PZ = 128


def circulant(tap_row, period):
    places = jnp.arange(period, dtype=jnp.int32)
    offsets = jnp.arange(9, dtype=jnp.int32) - 4
    target = (places[None, :, None] + offsets[:, None, None]) % period
    onehot = (target == places[None, None, :]).astype(jnp.float32)
    return jnp.einsum("k,kxa->xa", tap_row, onehot, precision=lax.Precision.HIGHEST)


def split_three(matrix):
    high = lax.reduce_precision(matrix, exponent_bits=8, mantissa_bits=7)
    rest = matrix - high
    mid = lax.reduce_precision(rest, exponent_bits=8, mantissa_bits=7)
    low = rest - mid
    return jnp.concatenate([high, mid, low], axis=1).astype(jnp.bfloat16)


def filter_kernel(taps_ref, span_ref, planes_ref, out_ref, gram_ref, spread_ref):
    taps = taps_ref.shape[1]
    reach = (taps - 1) // 2
    span = span_ref[...]

    @pl.when(pl.program_id(0) == 0)
    def _():
        gram_ref[...] = jnp.zeros(gram_ref.shape, jnp.float32)

    for x in range(PX):
        parts = jnp.dot(planes_ref[x], span, preferred_element_type=jnp.float32)
        spread_ref[x] = parts[:, :PZ] + parts[:, PZ : 2 * PZ] + parts[:, 2 * PZ :]
    for x in range(PX):
        acc = taps_ref[0, 0] * spread_ref[(x - reach) % PX]
        for k in range(1, taps):
            acc = acc + taps_ref[0, k] * spread_ref[(x + k - reach) % PX]
        out_ref[:, x * PZ : (x + 1) * PZ] = acc
    block = out_ref[...]
    gram_ref[...] += lax.dot_general(
        block,
        block,
        (((1,), (1,)), ((), ())),
        precision=lax.Precision.HIGHEST,
        preferred_element_type=jnp.float32,
    )


def filter_planes(planes, filter_taps):
    count = planes.shape[1]
    span = split_three(circulant(filter_taps[1], PZ).T)
    return pl.pallas_call(
        filter_kernel,
        grid=(count // SNAP,),
        in_specs=[
            pl.BlockSpec(memory_space=pltpu.SMEM),
            pl.BlockSpec((PZ, 3 * PZ), lambda i: (0, 0)),
            pl.BlockSpec((PX, SNAP, PZ), lambda i: (0, i, 0)),
        ],
        out_specs=[
            pl.BlockSpec((SNAP, PX * PZ), lambda i: (i, 0)),
            pl.BlockSpec((SNAP, SNAP), lambda i: (0, 0)),
        ],
        out_shape=[
            jax.ShapeDtypeStruct((count, PX * PZ), jnp.float32),
            jax.ShapeDtypeStruct((SNAP, SNAP), jnp.float32),
        ],
        scratch_shapes=[pltpu.VMEM((PX, SNAP, PZ), jnp.float32)],
    )(filter_taps, span, planes)


def basis_kernel(inv_ref, matrix_ref, basis_ref, gram_ref):
    @pl.when(pl.program_id(0) == 0)
    def _():
        gram_ref[...] = jnp.zeros(gram_ref.shape, jnp.float32)

    basis = jnp.dot(
        inv_ref[...],
        matrix_ref[...],
        precision=lax.Precision.HIGHEST,
        preferred_element_type=jnp.float32,
    )
    basis_ref[...] = basis
    gram_ref[...] += lax.dot_general(
        basis,
        basis,
        (((1,), (1,)), ((), ())),
        precision=lax.Precision.HIGHEST,
        preferred_element_type=jnp.float32,
    )


def basis_and_gram(inverse, matrix):
    count, width = matrix.shape
    size = inverse.shape[0]
    return pl.pallas_call(
        basis_kernel,
        grid=(count // size,),
        in_specs=[
            pl.BlockSpec((size, size), lambda i: (0, 0)),
            pl.BlockSpec((size, width), lambda i: (i, 0)),
        ],
        out_specs=[
            pl.BlockSpec((size, width), lambda i: (i, 0)),
            pl.BlockSpec((size, size), lambda i: (0, 0)),
        ],
        out_shape=[
            jax.ShapeDtypeStruct((count, width), jnp.float32),
            jax.ShapeDtypeStruct((size, size), jnp.float32),
        ],
    )(inverse, matrix)


def modes_kernel(inv_ref, basis_ref, modes_ref, *, scale):
    modes_ref[...] = (
        jnp.dot(
            inv_ref[...],
            basis_ref[...],
            precision=lax.Precision.HIGHEST,
            preferred_element_type=jnp.float32,
        )
        * scale
    )


def modes_of(inverse, basis, scale):
    count, width = basis.shape
    size = inverse.shape[0]
    return pl.pallas_call(
        functools.partial(modes_kernel, scale=scale),
        grid=(count // size,),
        in_specs=[
            pl.BlockSpec((size, size), lambda i: (0, 0)),
            pl.BlockSpec((size, width), lambda i: (i, 0)),
        ],
        out_specs=pl.BlockSpec((size, width), lambda i: (i, 0)),
        out_shape=jax.ShapeDtypeStruct((count, width), jnp.float32),
    )(inverse, basis)


def swap_kernel(planes_ref, records_ref):
    records_ref[...] = pltpu.einshape("akb->kab", planes_ref[...])


def planes_to_records(planes, rows=256):
    width, count, lanes = planes.shape
    return pl.pallas_call(
        swap_kernel,
        grid=(count // rows,),
        in_specs=[pl.BlockSpec((width, rows, lanes), lambda i: (0, i, 0))],
        out_specs=pl.BlockSpec((rows, width, lanes), lambda i: (i, 0, 0)),
        out_shape=jax.ShapeDtypeStruct((count, width, lanes), planes.dtype),
    )(planes)


def doubling_inverse(lower):
    size = lower.shape[0]
    row = lax.broadcasted_iota(jnp.int32, lower.shape, 0)
    col = lax.broadcasted_iota(jnp.int32, lower.shape, 1)
    inverse = jnp.where(row == col, 1.0 / lower, 0.0)
    level = 0
    while (1 << level) < size:
        same_pair = lax.shift_right_logical(row, level + 1) == lax.shift_right_logical(col, level + 1)
        other_half = lax.shift_right_logical(row, level) != lax.shift_right_logical(col, level)
        coupling = jnp.where(same_pair & other_half, lower, 0.0)
        step = jnp.dot(
            inverse, coupling, precision=lax.Precision.HIGHEST, preferred_element_type=jnp.float32
        )
        inverse = inverse - jnp.dot(
            step, inverse, precision=lax.Precision.HIGHEST, preferred_element_type=jnp.float32
        )
        level += 1
    return inverse


def nt_dot(a, b):
    return lax.dot_general(
        a, b, (((1,), (1,)), ((), ())), precision=lax.Precision.HIGHEST,
        preferred_element_type=jnp.float32,
    )


def nn_dot(a, b):
    return jnp.dot(a, b, precision=lax.Precision.HIGHEST, preferred_element_type=jnp.float32)


def lower_part(square):
    row = lax.broadcasted_iota(jnp.int32, square.shape, 0)
    col = lax.broadcasted_iota(jnp.int32, square.shape, 1)
    return jnp.where(row >= col, square, 0.0)


def first_half_kernel(lower_a_ref, gram_ref, inv_a_ref, lower_b_ref, rest_ref):
    half = lower_a_ref.shape[0]
    inv_a = doubling_inverse(lower_part(lower_a_ref[...]))
    inv_a_ref[...] = inv_a
    lower_b = nt_dot(gram_ref[half:, :half], inv_a)
    lower_b_ref[...] = lower_b
    rest_ref[...] = gram_ref[half:, half:] - nt_dot(lower_b, lower_b)


def second_half_kernel(lower_a_ref, lower_b_ref, lower_c_ref, inv_a_ref, lower_ref, inverse_ref):
    half = lower_a_ref.shape[0]
    lower_c = lower_part(lower_c_ref[...])
    inv_c = doubling_inverse(lower_c)
    inv_a = inv_a_ref[...]
    zero = jnp.zeros((half, half), jnp.float32)
    lower_ref[:half, :half] = lower_part(lower_a_ref[...])
    lower_ref[:half, half:] = zero
    lower_ref[half:, :half] = lower_b_ref[...]
    lower_ref[half:, half:] = lower_c
    inverse_ref[:half, :half] = inv_a
    inverse_ref[:half, half:] = zero
    inverse_ref[half:, :half] = -nn_dot(inv_c, nn_dot(lower_b_ref[...], inv_a))
    inverse_ref[half:, half:] = inv_c


def gram_of(matrix):
    return lax.dot_general(
        matrix,
        matrix,
        (((1,), (1,)), ((), ())),
        precision=lax.Precision.HIGHEST,
        preferred_element_type=jnp.float32,
    )


def high_dot(a, b, dims):
    return lax.dot_general(
        a, b, (dims, ((), ())), precision=lax.Precision.HIGHEST, preferred_element_type=jnp.float32
    )


def factor_and_inverse(gram):
    size = gram.shape[0]
    half = size // 2
    gram = (gram + gram.T) / 2
    lower_a = lax.linalg.cholesky_p.bind(gram[:half, :half])
    square = jax.ShapeDtypeStruct((half, half), jnp.float32)
    inv_a, lower_b, rest = pl.pallas_call(
        first_half_kernel, out_shape=[square, square, square]
    )(lower_a, gram)
    lower_c = lax.linalg.cholesky_p.bind(rest)
    full = jax.ShapeDtypeStruct((size, size), jnp.float32)
    lower, inverse = pl.pallas_call(
        second_half_kernel, out_shape=[full, full]
    )(lower_a, lower_b, lower_c, inv_a)
    return lower, inverse


def sum_over_devices(part, axes, devices_all):
    rows = part.reshape(devices_all, -1)
    rows = lax.all_to_all(rows, axes, 0, 0, tiled=True)
    total = jnp.sum(rows, axis=0, keepdims=True)
    total = jnp.broadcast_to(total, rows.shape)
    total = lax.all_to_all(total, axes, 0, 0, tiled=True)
    return total.reshape(part.shape)


def local(records, record_owner, record_field, filter_taps):
    devices_all = lax.axis_size(("gx", "gy"))
    rec_count = records.shape[0]
    cells = records.shape[1]
    capacity = 2 * (rec_count // devices_all)
    onehot = (record_owner[:, None] == jnp.arange(devices_all, dtype=jnp.int32)[None, :]).astype(
        jnp.int32
    )
    position = jnp.sum((jnp.cumsum(onehot, axis=0) - 1) * onehot, axis=1)
    slot = record_owner * capacity + position
    places = jnp.arange(devices_all * capacity, dtype=jnp.int32)
    pick = slot[None, :] == places[:, None]
    buffer = jnp.einsum(
        "kr,rab->akb",
        pick.astype(jnp.bfloat16),
        records.reshape(rec_count, PX, PZ),
        preferred_element_type=jnp.float32,
    ).astype(jnp.bfloat16)
    buffer = planes_to_records(buffer)
    labels = jnp.sum(jnp.where(pick, record_field[None, :] + 1, 0), axis=1) - 1
    arrived, arrived_labels = (
        lax.all_to_all(
            buffer.reshape(devices_all, capacity, PX, PZ),
            ("gx", "gy"),
            split_axis=0,
            concat_axis=0,
            tiled=True,
        ),
        lax.all_to_all(
            labels.reshape(devices_all, capacity),
            ("gx", "gy"),
            split_axis=0,
            concat_axis=0,
            tiled=True,
        ),
    )
    flat_data = arrived.reshape(devices_all * capacity, PX, PZ)
    flat_labels = arrived_labels.reshape(devices_all * capacity)
    target = (flat_labels % 3) * SNAP + flat_labels // 3
    target = jnp.where(flat_labels >= 0, target, -1)
    order = target[None, :] == jnp.arange(rec_count, dtype=jnp.int32)[:, None]
    planes = jnp.einsum(
        "tk,kab->atb", order.astype(jnp.bfloat16), flat_data, preferred_element_type=jnp.float32
    ).astype(jnp.bfloat16)
    fields, gram_one = filter_planes(planes, filter_taps)
    lower_one, inv_one = factor_and_inverse(sum_over_devices(gram_one, ("gx", "gy"), devices_all))
    basis_one, gram_two = basis_and_gram(inv_one, fields)
    lower_two, inv_two = factor_and_inverse(sum_over_devices(gram_two, ("gx", "gy"), devices_all))
    scale = math.sqrt(3.0 * cells * devices_all)
    modes = modes_of(inv_two, basis_one, scale).reshape(3, SNAP, cells)
    r_factor = (
        jnp.dot(
            lower_two.T,
            lower_one.T,
            precision=lax.Precision.HIGHEST,
            preferred_element_type=jnp.float32,
        )
        / scale
    )
    first_factor = lower_one.T / scale
    return (modes.transpose(1, 0, 2), r_factor, first_factor)


def solution(mesh):
    placed = (P(("gx", "gy"), None), P(("gx", "gy")), P(("gx", "gy")), P())
    return jax.shard_map(
        local,
        mesh=mesh,
        in_specs=placed,
        out_specs=(P(None, None, ("gx", "gy")), P(), P()),
        check_vma=False,
    )
```

```python
import functools
import math

import jax
import jax.numpy as jnp
from jax import lax
from jax.experimental import pallas as pl
from jax.experimental.pallas import tpu as pltpu
from jax.sharding import PartitionSpec as P

SNAP = 256
PX = 16
PZ = 128


def circulant(tap_row, period):
    places = jnp.arange(period, dtype=jnp.int32)
    offsets = jnp.arange(9, dtype=jnp.int32) - 4
    target = (places[None, :, None] + offsets[:, None, None]) % period
    onehot = (target == places[None, None, :]).astype(jnp.float32)
    return jnp.einsum("k,kxa->xa", tap_row, onehot, precision=lax.Precision.HIGHEST)


def split_three(matrix):
    high = lax.reduce_precision(matrix, exponent_bits=8, mantissa_bits=7)
    rest = matrix - high
    mid = lax.reduce_precision(rest, exponent_bits=8, mantissa_bits=7)
    low = rest - mid
    return jnp.concatenate([high, mid, low], axis=1).astype(jnp.bfloat16)


def filter_kernel(taps_ref, span_ref, planes_ref, out_ref, gram_ref, spread_ref):
    taps = taps_ref.shape[1]
    reach = (taps - 1) // 2
    span = span_ref[...]

    @pl.when(pl.program_id(0) == 0)
    def _():
        gram_ref[...] = jnp.zeros(gram_ref.shape, jnp.float32)

    for x in range(PX):
        parts = jnp.dot(planes_ref[x], span, preferred_element_type=jnp.float32)
        spread_ref[x] = parts[:, :PZ] + parts[:, PZ : 2 * PZ] + parts[:, 2 * PZ :]
    for x in range(PX):
        acc = taps_ref[0, 0] * spread_ref[(x - reach) % PX]
        for k in range(1, taps):
            acc = acc + taps_ref[0, k] * spread_ref[(x + k - reach) % PX]
        out_ref[:, x * PZ : (x + 1) * PZ] = acc
    block = out_ref[...]
    gram_ref[...] += lax.dot_general(
        block,
        block,
        (((1,), (1,)), ((), ())),
        precision=lax.Precision.HIGHEST,
        preferred_element_type=jnp.float32,
    )


def filter_planes(planes, filter_taps):
    count = planes.shape[1]
    span = split_three(circulant(filter_taps[1], PZ).T)
    return pl.pallas_call(
        filter_kernel,
        grid=(count // SNAP,),
        in_specs=[
            pl.BlockSpec(memory_space=pltpu.SMEM),
            pl.BlockSpec((PZ, 3 * PZ), lambda i: (0, 0)),
            pl.BlockSpec((PX, SNAP, PZ), lambda i: (0, i, 0)),
        ],
        out_specs=[
            pl.BlockSpec((SNAP, PX * PZ), lambda i: (i, 0)),
            pl.BlockSpec((SNAP, SNAP), lambda i: (0, 0)),
        ],
        out_shape=[
            jax.ShapeDtypeStruct((count, PX * PZ), jnp.float32),
            jax.ShapeDtypeStruct((SNAP, SNAP), jnp.float32),
        ],
        scratch_shapes=[pltpu.VMEM((PX, SNAP, PZ), jnp.float32)],
    )(filter_taps, span, planes)


def basis_kernel(inv_ref, matrix_ref, basis_ref, gram_ref):
    half = inv_ref.shape[0] // 2

    @pl.when(pl.program_id(0) == 0)
    def _():
        gram_ref[...] = jnp.zeros(gram_ref.shape, jnp.float32)

    top = nn_dot(inv_ref[:half, :half], matrix_ref[:half])
    bottom = nn_dot(inv_ref[half:, :half], matrix_ref[:half]) + nn_dot(
        inv_ref[half:, half:], matrix_ref[half:]
    )
    basis_ref[:half] = top
    basis_ref[half:] = bottom
    gram_ref[:half, :half] += nt_dot(top, top)
    gram_ref[half:, :half] += nt_dot(bottom, top)
    gram_ref[half:, half:] += nt_dot(bottom, bottom)


def basis_and_gram(inverse, matrix):
    count, width = matrix.shape
    size = inverse.shape[0]
    return pl.pallas_call(
        basis_kernel,
        grid=(count // size,),
        in_specs=[
            pl.BlockSpec((size, size), lambda i: (0, 0)),
            pl.BlockSpec((size, width), lambda i: (i, 0)),
        ],
        out_specs=[
            pl.BlockSpec((size, width), lambda i: (i, 0)),
            pl.BlockSpec((size, size), lambda i: (0, 0)),
        ],
        out_shape=[
            jax.ShapeDtypeStruct((count, width), jnp.float32),
            jax.ShapeDtypeStruct((size, size), jnp.float32),
        ],
    )(inverse, matrix)


def modes_kernel(inv_ref, basis_ref, modes_ref, *, scale):
    half = inv_ref.shape[0] // 2
    modes_ref[:half] = nn_dot(inv_ref[:half, :half], basis_ref[:half]) * scale
    modes_ref[half:] = (
        nn_dot(inv_ref[half:, :half], basis_ref[:half])
        + nn_dot(inv_ref[half:, half:], basis_ref[half:])
    ) * scale


def modes_of(inverse, basis, scale):
    count, width = basis.shape
    size = inverse.shape[0]
    return pl.pallas_call(
        functools.partial(modes_kernel, scale=scale),
        grid=(count // size,),
        in_specs=[
            pl.BlockSpec((size, size), lambda i: (0, 0)),
            pl.BlockSpec((size, width), lambda i: (i, 0)),
        ],
        out_specs=pl.BlockSpec((size, width), lambda i: (i, 0)),
        out_shape=jax.ShapeDtypeStruct((count, width), jnp.float32),
    )(inverse, basis)


def swap_kernel(planes_ref, records_ref):
    records_ref[...] = pltpu.einshape("akb->kab", planes_ref[...])


def planes_to_records(planes, rows=256):
    width, count, lanes = planes.shape
    return pl.pallas_call(
        swap_kernel,
        grid=(count // rows,),
        in_specs=[pl.BlockSpec((width, rows, lanes), lambda i: (0, i, 0))],
        out_specs=pl.BlockSpec((rows, width, lanes), lambda i: (i, 0, 0)),
        out_shape=jax.ShapeDtypeStruct((count, width, lanes), planes.dtype),
    )(planes)


def doubling_inverse(lower):
    size = lower.shape[0]
    row = lax.broadcasted_iota(jnp.int32, lower.shape, 0)
    col = lax.broadcasted_iota(jnp.int32, lower.shape, 1)
    inverse = jnp.where(row == col, 1.0 / lower, 0.0)
    level = 0
    while (1 << level) < size:
        same_pair = lax.shift_right_logical(row, level + 1) == lax.shift_right_logical(col, level + 1)
        other_half = lax.shift_right_logical(row, level) != lax.shift_right_logical(col, level)
        coupling = jnp.where(same_pair & other_half, lower, 0.0)
        step = jnp.dot(
            inverse, coupling, precision=lax.Precision.HIGHEST, preferred_element_type=jnp.float32
        )
        inverse = inverse - jnp.dot(
            step, inverse, precision=lax.Precision.HIGHEST, preferred_element_type=jnp.float32
        )
        level += 1
    return inverse


def nt_dot(a, b):
    return lax.dot_general(
        a, b, (((1,), (1,)), ((), ())), precision=lax.Precision.HIGHEST,
        preferred_element_type=jnp.float32,
    )


def nn_dot(a, b):
    return jnp.dot(a, b, precision=lax.Precision.HIGHEST, preferred_element_type=jnp.float32)


def lower_part(square):
    row = lax.broadcasted_iota(jnp.int32, square.shape, 0)
    col = lax.broadcasted_iota(jnp.int32, square.shape, 1)
    return jnp.where(row >= col, square, 0.0)


def first_half_kernel(lower_a_ref, gram_ref, inv_a_ref, lower_b_ref, rest_ref):
    half = lower_a_ref.shape[0]
    inv_a = doubling_inverse(lower_part(lower_a_ref[...]))
    inv_a_ref[...] = inv_a
    lower_b = nt_dot(gram_ref[half:, :half], inv_a)
    lower_b_ref[...] = lower_b
    far = gram_ref[half:, half:]
    rest_ref[...] = (far + far.T) / 2 - nt_dot(lower_b, lower_b)


def second_half_kernel(lower_a_ref, lower_b_ref, lower_c_ref, inv_a_ref, lower_ref, inverse_ref):
    half = lower_a_ref.shape[0]
    lower_c = lower_part(lower_c_ref[...])
    inv_c = doubling_inverse(lower_c)
    inv_a = inv_a_ref[...]
    zero = jnp.zeros((half, half), jnp.float32)
    lower_ref[:half, :half] = lower_part(lower_a_ref[...])
    lower_ref[:half, half:] = zero
    lower_ref[half:, :half] = lower_b_ref[...]
    lower_ref[half:, half:] = lower_c
    inverse_ref[:half, :half] = inv_a
    inverse_ref[:half, half:] = zero
    inverse_ref[half:, :half] = -nn_dot(inv_c, nn_dot(lower_b_ref[...], inv_a))
    inverse_ref[half:, half:] = inv_c


def gram_of(matrix):
    return lax.dot_general(
        matrix,
        matrix,
        (((1,), (1,)), ((), ())),
        precision=lax.Precision.HIGHEST,
        preferred_element_type=jnp.float32,
    )


def high_dot(a, b, dims):
    return lax.dot_general(
        a, b, (dims, ((), ())), precision=lax.Precision.HIGHEST, preferred_element_type=jnp.float32
    )


def factor_and_inverse(gram):
    size = gram.shape[0]
    half = size // 2
    corner = gram[:half, :half]
    lower_a = lax.linalg.cholesky_p.bind((corner + corner.T) / 2)
    square = jax.ShapeDtypeStruct((half, half), jnp.float32)
    inv_a, lower_b, rest = pl.pallas_call(
        first_half_kernel, out_shape=[square, square, square]
    )(lower_a, gram)
    lower_c = lax.linalg.cholesky_p.bind(rest)
    full = jax.ShapeDtypeStruct((size, size), jnp.float32)
    lower, inverse = pl.pallas_call(
        second_half_kernel, out_shape=[full, full]
    )(lower_a, lower_b, lower_c, inv_a)
    return lower, inverse


def sum_over_devices(part, axes, devices_all):
    rows = part.reshape(devices_all, -1)
    rows = lax.all_to_all(rows, axes, 0, 0, tiled=True)
    total = jnp.sum(rows, axis=0, keepdims=True)
    total = jnp.broadcast_to(total, rows.shape)
    total = lax.all_to_all(total, axes, 0, 0, tiled=True)
    return total.reshape(part.shape)


def local(records, record_owner, record_field, filter_taps):
    devices_all = lax.axis_size(("gx", "gy"))
    rec_count = records.shape[0]
    cells = records.shape[1]
    capacity = 2 * (rec_count // devices_all)
    onehot = (record_owner[:, None] == jnp.arange(devices_all, dtype=jnp.int32)[None, :]).astype(
        jnp.int32
    )
    position = jnp.sum((jnp.cumsum(onehot, axis=0) - 1) * onehot, axis=1)
    slot = record_owner * capacity + position
    places = jnp.arange(devices_all * capacity, dtype=jnp.int32)
    pick = slot[None, :] == places[:, None]
    buffer = jnp.einsum(
        "kr,rab->akb",
        pick.astype(jnp.bfloat16),
        records.reshape(rec_count, PX, PZ),
        preferred_element_type=jnp.float32,
    ).astype(jnp.bfloat16)
    buffer = planes_to_records(buffer)
    labels = jnp.sum(jnp.where(pick, record_field[None, :] + 1, 0), axis=1) - 1
    arrived, arrived_labels = (
        lax.all_to_all(
            buffer.reshape(devices_all, capacity, PX, PZ),
            ("gx", "gy"),
            split_axis=0,
            concat_axis=0,
            tiled=True,
        ),
        lax.all_to_all(
            labels.reshape(devices_all, capacity),
            ("gx", "gy"),
            split_axis=0,
            concat_axis=0,
            tiled=True,
        ),
    )
    flat_data = arrived.reshape(devices_all * capacity, PX, PZ)
    flat_labels = arrived_labels.reshape(devices_all * capacity)
    target = (flat_labels % 3) * SNAP + flat_labels // 3
    target = jnp.where(flat_labels >= 0, target, -1)
    order = target[None, :] == jnp.arange(rec_count, dtype=jnp.int32)[:, None]
    planes = jnp.einsum(
        "tk,kab->atb", order.astype(jnp.bfloat16), flat_data, preferred_element_type=jnp.float32
    ).astype(jnp.bfloat16)
    fields, gram_one = filter_planes(planes, filter_taps)
    lower_one, inv_one = factor_and_inverse(sum_over_devices(gram_one, ("gx", "gy"), devices_all))
    basis_one, gram_two = basis_and_gram(inv_one, fields)
    lower_two, inv_two = factor_and_inverse(sum_over_devices(gram_two, ("gx", "gy"), devices_all))
    scale = math.sqrt(3.0 * cells * devices_all)
    modes = modes_of(inv_two, basis_one, scale).reshape(3, SNAP, cells)
    r_factor = (
        jnp.dot(
            lower_two.T,
            lower_one.T,
            precision=lax.Precision.HIGHEST,
            preferred_element_type=jnp.float32,
        )
        / scale
    )
    first_factor = lower_one.T / scale
    return (modes.transpose(1, 0, 2), r_factor, first_factor)


def solution(mesh):
    placed = (P(("gx", "gy"), None), P(("gx", "gy")), P(("gx", "gy")), P())
    return jax.shard_map(
        local,
        mesh=mesh,
        in_specs=placed,
        out_specs=(P(None, None, ("gx", "gy")), P(), P()),
        check_vma=False,
    )
```

```python
import functools
import math

import jax
import jax.numpy as jnp
from jax import lax
from jax.experimental import pallas as pl
from jax.experimental.pallas import tpu as pltpu
from jax.sharding import PartitionSpec as P

SNAP = 256
PX = 16
PZ = 128


def circulant(tap_row, period):
    places = jnp.arange(period, dtype=jnp.int32)
    offsets = jnp.arange(9, dtype=jnp.int32) - 4
    target = (places[None, :, None] + offsets[:, None, None]) % period
    onehot = (target == places[None, None, :]).astype(jnp.float32)
    return jnp.einsum("k,kxa->xa", tap_row, onehot, precision=lax.Precision.HIGHEST)


def split_three(matrix):
    high = lax.reduce_precision(matrix, exponent_bits=8, mantissa_bits=7)
    rest = matrix - high
    mid = lax.reduce_precision(rest, exponent_bits=8, mantissa_bits=7)
    low = rest - mid
    return jnp.concatenate([high, mid, low], axis=1).astype(jnp.bfloat16)


def filter_kernel(taps_ref, span_ref, planes_ref, out_ref, gram_ref, spread_ref):
    taps = taps_ref.shape[1]
    reach = (taps - 1) // 2
    span = span_ref[...]

    @pl.when(pl.program_id(0) == 0)
    def _():
        gram_ref[...] = jnp.zeros(gram_ref.shape, jnp.float32)

    for x in range(PX):
        parts = jnp.dot(planes_ref[x], span, preferred_element_type=jnp.float32)
        spread_ref[x] = parts[:, :PZ] + parts[:, PZ : 2 * PZ] + parts[:, 2 * PZ :]
    for x in range(PX):
        acc = taps_ref[0, 0] * spread_ref[(x - reach) % PX]
        for k in range(1, taps):
            acc = acc + taps_ref[0, k] * spread_ref[(x + k - reach) % PX]
        out_ref[:, x * PZ : (x + 1) * PZ] = acc
    block = out_ref[...]
    gram_ref[...] += lax.dot_general(
        block,
        block,
        (((1,), (1,)), ((), ())),
        precision=lax.Precision.HIGHEST,
        preferred_element_type=jnp.float32,
    )


def filter_planes(planes, filter_taps):
    count = planes.shape[1]
    span = split_three(circulant(filter_taps[1], PZ).T)
    return pl.pallas_call(
        filter_kernel,
        grid=(count // SNAP,),
        in_specs=[
            pl.BlockSpec(memory_space=pltpu.SMEM),
            pl.BlockSpec((PZ, 3 * PZ), lambda i: (0, 0)),
            pl.BlockSpec((PX, SNAP, PZ), lambda i: (0, i, 0)),
        ],
        out_specs=[
            pl.BlockSpec((SNAP, PX * PZ), lambda i: (i, 0)),
            pl.BlockSpec((SNAP, SNAP), lambda i: (0, 0)),
        ],
        out_shape=[
            jax.ShapeDtypeStruct((count, PX * PZ), jnp.float32),
            jax.ShapeDtypeStruct((SNAP, SNAP), jnp.float32),
        ],
        scratch_shapes=[pltpu.VMEM((PX, SNAP, PZ), jnp.float32)],
    )(filter_taps, span, planes)


def basis_kernel(inv_ref, matrix_ref, basis_ref, gram_ref):
    @pl.when(pl.program_id(0) == 0)
    def _():
        gram_ref[...] = jnp.zeros(gram_ref.shape, jnp.float32)

    basis = jnp.dot(
        inv_ref[...],
        matrix_ref[...],
        precision=lax.Precision.HIGHEST,
        preferred_element_type=jnp.float32,
    )
    basis_ref[...] = basis
    gram_ref[...] += lax.dot_general(
        basis,
        basis,
        (((1,), (1,)), ((), ())),
        precision=lax.Precision.HIGHEST,
        preferred_element_type=jnp.float32,
    )


def basis_and_gram(inverse, matrix):
    count, width = matrix.shape
    size = inverse.shape[0]
    return pl.pallas_call(
        basis_kernel,
        grid=(count // size,),
        in_specs=[
            pl.BlockSpec((size, size), lambda i: (0, 0)),
            pl.BlockSpec((size, width), lambda i: (i, 0)),
        ],
        out_specs=[
            pl.BlockSpec((size, width), lambda i: (i, 0)),
            pl.BlockSpec((size, size), lambda i: (0, 0)),
        ],
        out_shape=[
            jax.ShapeDtypeStruct((count, width), jnp.float32),
            jax.ShapeDtypeStruct((size, size), jnp.float32),
        ],
    )(inverse, matrix)


def modes_kernel(inv_ref, basis_ref, modes_ref, *, scale):
    modes_ref[...] = (
        jnp.dot(
            inv_ref[...],
            basis_ref[...],
            precision=lax.Precision.HIGHEST,
            preferred_element_type=jnp.float32,
        )
        * scale
    )


def modes_of(inverse, basis, scale):
    count, width = basis.shape
    size = inverse.shape[0]
    return pl.pallas_call(
        functools.partial(modes_kernel, scale=scale),
        grid=(count // size,),
        in_specs=[
            pl.BlockSpec((size, size), lambda i: (0, 0)),
            pl.BlockSpec((size, width), lambda i: (i, 0)),
        ],
        out_specs=pl.BlockSpec((size, width), lambda i: (i, 0)),
        out_shape=jax.ShapeDtypeStruct((count, width), jnp.float32),
    )(inverse, basis)


def route_kernel(slot_ref, records_ref, buffer_ref, planes_ref):
    rows = buffer_ref.shape[0]
    first = pl.program_id(0) * rows
    places = first + lax.broadcasted_iota(jnp.int32, (rows, slot_ref.shape[1]), 0)
    pick = (slot_ref[...] == places).astype(jnp.bfloat16)
    for x in range(PX):
        planes_ref[x] = jnp.dot(
            pick, records_ref[:, x * PZ : (x + 1) * PZ], preferred_element_type=jnp.float32
        ).astype(jnp.bfloat16)
    buffer_ref[...] = pltpu.einshape("akb->kab", planes_ref[...])


def route_records(slot, records, slots, rows=256):
    count, width = records.shape
    return pl.pallas_call(
        route_kernel,
        grid=(slots // rows,),
        in_specs=[
            pl.BlockSpec((1, count), lambda i: (0, 0)),
            pl.BlockSpec((count, width), lambda i: (0, 0)),
        ],
        out_specs=pl.BlockSpec((rows, PX, PZ), lambda i: (i, 0, 0)),
        out_shape=jax.ShapeDtypeStruct((slots, PX, PZ), jnp.bfloat16),
        scratch_shapes=[pltpu.VMEM((PX, rows, PZ), jnp.bfloat16)],
    )(slot.reshape(1, count), records)


def swap_kernel(planes_ref, records_ref):
    records_ref[...] = pltpu.einshape("akb->kab", planes_ref[...])


def planes_to_records(planes, rows=256):
    width, count, lanes = planes.shape
    return pl.pallas_call(
        swap_kernel,
        grid=(count // rows,),
        in_specs=[pl.BlockSpec((width, rows, lanes), lambda i: (0, i, 0))],
        out_specs=pl.BlockSpec((rows, width, lanes), lambda i: (i, 0, 0)),
        out_shape=jax.ShapeDtypeStruct((count, width, lanes), planes.dtype),
    )(planes)


def doubling_inverse(lower):
    size = lower.shape[0]
    row = lax.broadcasted_iota(jnp.int32, lower.shape, 0)
    col = lax.broadcasted_iota(jnp.int32, lower.shape, 1)
    inverse = jnp.where(row == col, 1.0 / lower, 0.0)
    level = 0
    while (1 << level) < size:
        same_pair = lax.shift_right_logical(row, level + 1) == lax.shift_right_logical(col, level + 1)
        other_half = lax.shift_right_logical(row, level) != lax.shift_right_logical(col, level)
        coupling = jnp.where(same_pair & other_half, lower, 0.0)
        step = jnp.dot(
            inverse, coupling, precision=lax.Precision.HIGHEST, preferred_element_type=jnp.float32
        )
        inverse = inverse - jnp.dot(
            step, inverse, precision=lax.Precision.HIGHEST, preferred_element_type=jnp.float32
        )
        level += 1
    return inverse


def nt_dot(a, b):
    return lax.dot_general(
        a, b, (((1,), (1,)), ((), ())), precision=lax.Precision.HIGHEST,
        preferred_element_type=jnp.float32,
    )


def nn_dot(a, b):
    return jnp.dot(a, b, precision=lax.Precision.HIGHEST, preferred_element_type=jnp.float32)


def first_half_kernel(lower_a_ref, gram_ref, inv_a_ref, lower_b_ref, rest_ref):
    half = lower_a_ref.shape[0]
    inv_a = doubling_inverse(lower_a_ref[...])
    inv_a_ref[...] = inv_a
    lower_b = nt_dot(gram_ref[half:, :half], inv_a)
    lower_b_ref[...] = lower_b
    rest_ref[...] = gram_ref[half:, half:] - nt_dot(lower_b, lower_b)


def second_half_kernel(lower_a_ref, lower_b_ref, lower_c_ref, inv_a_ref, lower_ref, inverse_ref):
    half = lower_a_ref.shape[0]
    inv_c = doubling_inverse(lower_c_ref[...])
    inv_a = inv_a_ref[...]
    zero = jnp.zeros((half, half), jnp.float32)
    lower_ref[:half, :half] = lower_a_ref[...]
    lower_ref[:half, half:] = zero
    lower_ref[half:, :half] = lower_b_ref[...]
    lower_ref[half:, half:] = lower_c_ref[...]
    inverse_ref[:half, :half] = inv_a
    inverse_ref[:half, half:] = zero
    inverse_ref[half:, :half] = -nn_dot(inv_c, nn_dot(lower_b_ref[...], inv_a))
    inverse_ref[half:, half:] = inv_c


def gram_of(matrix):
    return lax.dot_general(
        matrix,
        matrix,
        (((1,), (1,)), ((), ())),
        precision=lax.Precision.HIGHEST,
        preferred_element_type=jnp.float32,
    )


def high_dot(a, b, dims):
    return lax.dot_general(
        a, b, (dims, ((), ())), precision=lax.Precision.HIGHEST, preferred_element_type=jnp.float32
    )


def factor_and_inverse(gram):
    size = gram.shape[0]
    half = size // 2
    gram = (gram + gram.T) / 2
    lower_a = lax.linalg.cholesky(gram[:half, :half], symmetrize_input=False)
    square = jax.ShapeDtypeStruct((half, half), jnp.float32)
    inv_a, lower_b, rest = pl.pallas_call(
        first_half_kernel, out_shape=[square, square, square]
    )(lower_a, gram)
    lower_c = lax.linalg.cholesky(rest, symmetrize_input=False)
    full = jax.ShapeDtypeStruct((size, size), jnp.float32)
    lower, inverse = pl.pallas_call(
        second_half_kernel, out_shape=[full, full]
    )(lower_a, lower_b, lower_c, inv_a)
    return lower, inverse


def sum_over_devices(part, axes, devices_all):
    rows = part.reshape(devices_all, -1)
    rows = lax.all_to_all(rows, axes, 0, 0, tiled=True)
    total = jnp.sum(rows, axis=0, keepdims=True)
    total = jnp.broadcast_to(total, rows.shape)
    total = lax.all_to_all(total, axes, 0, 0, tiled=True)
    return total.reshape(part.shape)


def local(records, record_owner, record_field, filter_taps):
    devices_all = lax.axis_size(("gx", "gy"))
    rec_count = records.shape[0]
    cells = records.shape[1]
    capacity = 2 * (rec_count // devices_all)
    onehot = (record_owner[:, None] == jnp.arange(devices_all, dtype=jnp.int32)[None, :]).astype(
        jnp.int32
    )
    position = jnp.sum((jnp.cumsum(onehot, axis=0) - 1) * onehot, axis=1)
    slot = record_owner * capacity + position
    places = jnp.arange(devices_all * capacity, dtype=jnp.int32)
    pick = slot[None, :] == places[:, None]
    buffer = route_records(slot, records, devices_all * capacity)
    labels = jnp.sum(jnp.where(pick, record_field[None, :] + 1, 0), axis=1) - 1
    arrived, arrived_labels = (
        lax.all_to_all(
            buffer.reshape(devices_all, capacity, PX, PZ),
            ("gx", "gy"),
            split_axis=0,
            concat_axis=0,
            tiled=True,
        ),
        lax.all_to_all(
            labels.reshape(devices_all, capacity),
            ("gx", "gy"),
            split_axis=0,
            concat_axis=0,
            tiled=True,
        ),
    )
    flat_data = arrived.reshape(devices_all * capacity, PX, PZ)
    flat_labels = arrived_labels.reshape(devices_all * capacity)
    target = (flat_labels % 3) * SNAP + flat_labels // 3
    target = jnp.where(flat_labels >= 0, target, -1)
    order = target[None, :] == jnp.arange(rec_count, dtype=jnp.int32)[:, None]
    planes = jnp.einsum(
        "tk,kab->atb", order.astype(jnp.bfloat16), flat_data, preferred_element_type=jnp.float32
    ).astype(jnp.bfloat16)
    fields, gram_one = filter_planes(planes, filter_taps)
    lower_one, inv_one = factor_and_inverse(sum_over_devices(gram_one, ("gx", "gy"), devices_all))
    basis_one, gram_two = basis_and_gram(inv_one, fields)
    lower_two, inv_two = factor_and_inverse(sum_over_devices(gram_two, ("gx", "gy"), devices_all))
    scale = math.sqrt(3.0 * cells * devices_all)
    modes = modes_of(inv_two, basis_one, scale).reshape(3, SNAP, cells)
    r_factor = (
        jnp.dot(
            lower_two.T,
            lower_one.T,
            precision=lax.Precision.HIGHEST,
            preferred_element_type=jnp.float32,
        )
        / scale
    )
    first_factor = lower_one.T / scale
    return (modes.transpose(1, 0, 2), r_factor, first_factor)


def solution(mesh):
    placed = (P(("gx", "gy"), None), P(("gx", "gy")), P(("gx", "gy")), P())
    return jax.shard_map(
        local,
        mesh=mesh,
        in_specs=placed,
        out_specs=(P(None, None, ("gx", "gy")), P(), P()),
        check_vma=False,
    )
```

```python
import functools
import math

import jax
import jax.numpy as jnp
from jax import lax
from jax.experimental import pallas as pl
from jax.experimental.pallas import tpu as pltpu
from jax.sharding import PartitionSpec as P

SNAP = 256
PX = 16
PZ = 128


def circulant(tap_row, period):
    places = jnp.arange(period, dtype=jnp.int32)
    offsets = jnp.arange(9, dtype=jnp.int32) - 4
    target = (places[None, :, None] + offsets[:, None, None]) % period
    onehot = (target == places[None, None, :]).astype(jnp.float32)
    return jnp.einsum("k,kxa->xa", tap_row, onehot, precision=lax.Precision.HIGHEST)


def split_three(matrix):
    high = lax.reduce_precision(matrix, exponent_bits=8, mantissa_bits=7)
    rest = matrix - high
    mid = lax.reduce_precision(rest, exponent_bits=8, mantissa_bits=7)
    low = rest - mid
    return jnp.concatenate([high, mid, low], axis=1).astype(jnp.bfloat16)


def filter_kernel(taps_ref, span_ref, planes_ref, out_ref, gram_ref, spread_ref):
    taps = taps_ref.shape[1]
    reach = (taps - 1) // 2
    span = span_ref[...]

    @pl.when(pl.program_id(0) == 0)
    def _():
        gram_ref[...] = jnp.zeros(gram_ref.shape, jnp.float32)

    for x in range(PX):
        parts = jnp.dot(planes_ref[x], span, preferred_element_type=jnp.float32)
        spread_ref[x] = parts[:, :PZ] + parts[:, PZ : 2 * PZ] + parts[:, 2 * PZ :]
    for x in range(PX):
        acc = taps_ref[0, 0] * spread_ref[(x - reach) % PX]
        for k in range(1, taps):
            acc = acc + taps_ref[0, k] * spread_ref[(x + k - reach) % PX]
        out_ref[:, x * PZ : (x + 1) * PZ] = acc
    block = out_ref[...]
    gram_ref[...] += lax.dot_general(
        block,
        block,
        (((1,), (1,)), ((), ())),
        precision=lax.Precision.HIGHEST,
        preferred_element_type=jnp.float32,
    )


def filter_planes(planes, filter_taps):
    count = planes.shape[1]
    span = split_three(circulant(filter_taps[1], PZ).T)
    return pl.pallas_call(
        filter_kernel,
        grid=(count // SNAP,),
        in_specs=[
            pl.BlockSpec(memory_space=pltpu.SMEM),
            pl.BlockSpec((PZ, 3 * PZ), lambda i: (0, 0)),
            pl.BlockSpec((PX, SNAP, PZ), lambda i: (0, i, 0)),
        ],
        out_specs=[
            pl.BlockSpec((SNAP, PX * PZ), lambda i: (i, 0)),
            pl.BlockSpec((SNAP, SNAP), lambda i: (0, 0)),
        ],
        out_shape=[
            jax.ShapeDtypeStruct((count, PX * PZ), jnp.float32),
            jax.ShapeDtypeStruct((SNAP, SNAP), jnp.float32),
        ],
        scratch_shapes=[pltpu.VMEM((PX, SNAP, PZ), jnp.float32)],
    )(filter_taps, span, planes)


def basis_kernel(inv_ref, matrix_ref, basis_ref, gram_ref):
    @pl.when(pl.program_id(0) == 0)
    def _():
        gram_ref[...] = jnp.zeros(gram_ref.shape, jnp.float32)

    basis = jnp.dot(
        inv_ref[...],
        matrix_ref[...],
        precision=lax.Precision.HIGHEST,
        preferred_element_type=jnp.float32,
    )
    basis_ref[...] = basis
    gram_ref[...] += lax.dot_general(
        basis,
        basis,
        (((1,), (1,)), ((), ())),
        precision=lax.Precision.HIGHEST,
        preferred_element_type=jnp.float32,
    )


def basis_and_gram(inverse, matrix):
    count, width = matrix.shape
    size = inverse.shape[0]
    return pl.pallas_call(
        basis_kernel,
        grid=(count // size,),
        in_specs=[
            pl.BlockSpec((size, size), lambda i: (0, 0)),
            pl.BlockSpec((size, width), lambda i: (i, 0)),
        ],
        out_specs=[
            pl.BlockSpec((size, width), lambda i: (i, 0)),
            pl.BlockSpec((size, size), lambda i: (0, 0)),
        ],
        out_shape=[
            jax.ShapeDtypeStruct((count, width), jnp.float32),
            jax.ShapeDtypeStruct((size, size), jnp.float32),
        ],
    )(inverse, matrix)


def modes_kernel(inv_ref, basis_ref, modes_ref, *, scale):
    modes_ref[...] = (
        jnp.dot(
            inv_ref[...],
            basis_ref[...],
            precision=lax.Precision.HIGHEST,
            preferred_element_type=jnp.float32,
        )
        * scale
    )


def modes_of(inverse, basis, scale):
    count, width = basis.shape
    size = inverse.shape[0]
    return pl.pallas_call(
        functools.partial(modes_kernel, scale=scale),
        grid=(count // size,),
        in_specs=[
            pl.BlockSpec((size, size), lambda i: (0, 0)),
            pl.BlockSpec((size, width), lambda i: (i, 0)),
        ],
        out_specs=pl.BlockSpec((size, width), lambda i: (i, 0)),
        out_shape=jax.ShapeDtypeStruct((count, width), jnp.float32),
    )(inverse, basis)


def route_kernel(slot_ref, records_ref, buffer_ref, planes_ref):
    rows = buffer_ref.shape[0]
    first = pl.program_id(0) * rows
    places = first + lax.broadcasted_iota(jnp.int32, (rows, slot_ref.shape[1]), 0)
    pick = (slot_ref[...] == places).astype(jnp.bfloat16)
    for x in range(PX):
        planes_ref[x] = jnp.dot(
            pick, records_ref[:, x * PZ : (x + 1) * PZ], preferred_element_type=jnp.float32
        ).astype(jnp.bfloat16)
    buffer_ref[...] = pltpu.einshape("akb->kab", planes_ref[...])


def route_records(slot, records, slots, rows=512):
    count, width = records.shape
    return pl.pallas_call(
        route_kernel,
        grid=(slots // rows,),
        in_specs=[
            pl.BlockSpec((1, count), lambda i: (0, 0)),
            pl.BlockSpec((count, width), lambda i: (0, 0)),
        ],
        out_specs=pl.BlockSpec((rows, PX, PZ), lambda i: (i, 0, 0)),
        out_shape=jax.ShapeDtypeStruct((slots, PX, PZ), jnp.bfloat16),
        scratch_shapes=[pltpu.VMEM((PX, rows, PZ), jnp.bfloat16)],
    )(slot.reshape(1, count), records)


def swap_kernel(planes_ref, records_ref):
    records_ref[...] = pltpu.einshape("akb->kab", planes_ref[...])


def planes_to_records(planes, rows=256):
    width, count, lanes = planes.shape
    return pl.pallas_call(
        swap_kernel,
        grid=(count // rows,),
        in_specs=[pl.BlockSpec((width, rows, lanes), lambda i: (0, i, 0))],
        out_specs=pl.BlockSpec((rows, width, lanes), lambda i: (i, 0, 0)),
        out_shape=jax.ShapeDtypeStruct((count, width, lanes), planes.dtype),
    )(planes)


def doubling_inverse(lower):
    size = lower.shape[0]
    row = lax.broadcasted_iota(jnp.int32, lower.shape, 0)
    col = lax.broadcasted_iota(jnp.int32, lower.shape, 1)
    inverse = jnp.where(row == col, 1.0 / lower, 0.0)
    level = 0
    while (1 << level) < size:
        same_pair = lax.shift_right_logical(row, level + 1) == lax.shift_right_logical(col, level + 1)
        other_half = lax.shift_right_logical(row, level) != lax.shift_right_logical(col, level)
        coupling = jnp.where(same_pair & other_half, lower, 0.0)
        step = jnp.dot(
            inverse, coupling, precision=lax.Precision.HIGHEST, preferred_element_type=jnp.float32
        )
        inverse = inverse - jnp.dot(
            step, inverse, precision=lax.Precision.HIGHEST, preferred_element_type=jnp.float32
        )
        level += 1
    return inverse


def nt_dot(a, b):
    return lax.dot_general(
        a, b, (((1,), (1,)), ((), ())), precision=lax.Precision.HIGHEST,
        preferred_element_type=jnp.float32,
    )


def nn_dot(a, b):
    return jnp.dot(a, b, precision=lax.Precision.HIGHEST, preferred_element_type=jnp.float32)


def first_half_kernel(lower_a_ref, gram_ref, inv_a_ref, lower_b_ref, rest_ref):
    half = lower_a_ref.shape[0]
    inv_a = doubling_inverse(lower_a_ref[...])
    inv_a_ref[...] = inv_a
    lower_b = nt_dot(gram_ref[half:, :half], inv_a)
    lower_b_ref[...] = lower_b
    rest_ref[...] = gram_ref[half:, half:] - nt_dot(lower_b, lower_b)


def second_half_kernel(lower_a_ref, lower_b_ref, lower_c_ref, inv_a_ref, lower_ref, inverse_ref):
    half = lower_a_ref.shape[0]
    inv_c = doubling_inverse(lower_c_ref[...])
    inv_a = inv_a_ref[...]
    zero = jnp.zeros((half, half), jnp.float32)
    lower_ref[:half, :half] = lower_a_ref[...]
    lower_ref[:half, half:] = zero
    lower_ref[half:, :half] = lower_b_ref[...]
    lower_ref[half:, half:] = lower_c_ref[...]
    inverse_ref[:half, :half] = inv_a
    inverse_ref[:half, half:] = zero
    inverse_ref[half:, :half] = -nn_dot(inv_c, nn_dot(lower_b_ref[...], inv_a))
    inverse_ref[half:, half:] = inv_c


def gram_of(matrix):
    return lax.dot_general(
        matrix,
        matrix,
        (((1,), (1,)), ((), ())),
        precision=lax.Precision.HIGHEST,
        preferred_element_type=jnp.float32,
    )


def high_dot(a, b, dims):
    return lax.dot_general(
        a, b, (dims, ((), ())), precision=lax.Precision.HIGHEST, preferred_element_type=jnp.float32
    )


def factor_and_inverse(gram):
    size = gram.shape[0]
    half = size // 2
    gram = (gram + gram.T) / 2
    lower_a = lax.linalg.cholesky(gram[:half, :half], symmetrize_input=False)
    square = jax.ShapeDtypeStruct((half, half), jnp.float32)
    inv_a, lower_b, rest = pl.pallas_call(
        first_half_kernel, out_shape=[square, square, square]
    )(lower_a, gram)
    lower_c = lax.linalg.cholesky(rest, symmetrize_input=False)
    full = jax.ShapeDtypeStruct((size, size), jnp.float32)
    lower, inverse = pl.pallas_call(
        second_half_kernel, out_shape=[full, full]
    )(lower_a, lower_b, lower_c, inv_a)
    return lower, inverse


def sum_over_devices(part, axes, devices_all):
    rows = part.reshape(devices_all, -1)
    rows = lax.all_to_all(rows, axes, 0, 0, tiled=True)
    total = jnp.sum(rows, axis=0, keepdims=True)
    total = jnp.broadcast_to(total, rows.shape)
    total = lax.all_to_all(total, axes, 0, 0, tiled=True)
    return total.reshape(part.shape)


def local(records, record_owner, record_field, filter_taps):
    devices_all = lax.axis_size(("gx", "gy"))
    rec_count = records.shape[0]
    cells = records.shape[1]
    capacity = 2 * (rec_count // devices_all)
    onehot = (record_owner[:, None] == jnp.arange(devices_all, dtype=jnp.int32)[None, :]).astype(
        jnp.int32
    )
    position = jnp.sum((jnp.cumsum(onehot, axis=0) - 1) * onehot, axis=1)
    slot = record_owner * capacity + position
    places = jnp.arange(devices_all * capacity, dtype=jnp.int32)
    pick = slot[None, :] == places[:, None]
    buffer = route_records(slot, records, devices_all * capacity)
    labels = jnp.sum(jnp.where(pick, record_field[None, :] + 1, 0), axis=1) - 1
    arrived, arrived_labels = (
        lax.all_to_all(
            buffer.reshape(devices_all, capacity, PX, PZ),
            ("gx", "gy"),
            split_axis=0,
            concat_axis=0,
            tiled=True,
        ),
        lax.all_to_all(
            labels.reshape(devices_all, capacity),
            ("gx", "gy"),
            split_axis=0,
            concat_axis=0,
            tiled=True,
        ),
    )
    flat_data = arrived.reshape(devices_all * capacity, PX, PZ)
    flat_labels = arrived_labels.reshape(devices_all * capacity)
    target = (flat_labels % 3) * SNAP + flat_labels // 3
    target = jnp.where(flat_labels >= 0, target, -1)
    order = target[None, :] == jnp.arange(rec_count, dtype=jnp.int32)[:, None]
    planes = jnp.einsum(
        "tk,kab->atb", order.astype(jnp.bfloat16), flat_data, preferred_element_type=jnp.float32
    ).astype(jnp.bfloat16)
    fields, gram_one = filter_planes(planes, filter_taps)
    lower_one, inv_one = factor_and_inverse(sum_over_devices(gram_one, ("gx", "gy"), devices_all))
    basis_one, gram_two = basis_and_gram(inv_one, fields)
    lower_two, inv_two = factor_and_inverse(sum_over_devices(gram_two, ("gx", "gy"), devices_all))
    scale = math.sqrt(3.0 * cells * devices_all)
    modes = modes_of(inv_two, basis_one, scale).reshape(3, SNAP, cells)
    r_factor = (
        jnp.dot(
            lower_two.T,
            lower_one.T,
            precision=lax.Precision.HIGHEST,
            preferred_element_type=jnp.float32,
        )
        / scale
    )
    first_factor = lower_one.T / scale
    return (modes.transpose(1, 0, 2), r_factor, first_factor)


def solution(mesh):
    placed = (P(("gx", "gy"), None), P(("gx", "gy")), P(("gx", "gy")), P())
    return jax.shard_map(
        local,
        mesh=mesh,
        in_specs=placed,
        out_specs=(P(None, None, ("gx", "gy")), P(), P()),
        check_vma=False,
    )
```

```python
import functools
import math

import jax
import jax.numpy as jnp
from jax import lax
from jax.experimental import pallas as pl
from jax.experimental.pallas import tpu as pltpu
from jax.sharding import PartitionSpec as P

SNAP = 256
PX = 16
PZ = 128


def circulant(tap_row, period):
    places = jnp.arange(period, dtype=jnp.int32)
    offsets = jnp.arange(9, dtype=jnp.int32) - 4
    target = (places[None, :, None] + offsets[:, None, None]) % period
    onehot = (target == places[None, None, :]).astype(jnp.float32)
    return jnp.einsum("k,kxa->xa", tap_row, onehot, precision=lax.Precision.HIGHEST)


def split_three(matrix):
    high = lax.reduce_precision(matrix, exponent_bits=8, mantissa_bits=7)
    rest = matrix - high
    mid = lax.reduce_precision(rest, exponent_bits=8, mantissa_bits=7)
    low = rest - mid
    return jnp.concatenate([high, mid, low], axis=1).astype(jnp.bfloat16)


def filter_kernel(taps_ref, span_ref, planes_ref, out_ref, gram_ref, spread_ref):
    taps = taps_ref.shape[1]
    reach = (taps - 1) // 2
    span = span_ref[...]

    @pl.when(pl.program_id(0) == 0)
    def _():
        gram_ref[...] = jnp.zeros(gram_ref.shape, jnp.float32)

    for x in range(PX):
        parts = jnp.dot(planes_ref[x], span, preferred_element_type=jnp.float32)
        spread_ref[x] = parts[:, :PZ] + parts[:, PZ : 2 * PZ] + parts[:, 2 * PZ :]
    for x in range(PX):
        acc = taps_ref[0, 0] * spread_ref[(x - reach) % PX]
        for k in range(1, taps):
            acc = acc + taps_ref[0, k] * spread_ref[(x + k - reach) % PX]
        out_ref[:, x * PZ : (x + 1) * PZ] = acc
    block = out_ref[...]
    gram_ref[...] += lax.dot_general(
        block,
        block,
        (((1,), (1,)), ((), ())),
        precision=lax.Precision.HIGHEST,
        preferred_element_type=jnp.float32,
    )


def filter_planes(planes, filter_taps):
    count = planes.shape[1]
    span = split_three(circulant(filter_taps[1], PZ).T)
    return pl.pallas_call(
        filter_kernel,
        grid=(count // SNAP,),
        in_specs=[
            pl.BlockSpec(memory_space=pltpu.SMEM),
            pl.BlockSpec((PZ, 3 * PZ), lambda i: (0, 0)),
            pl.BlockSpec((PX, SNAP, PZ), lambda i: (0, i, 0)),
        ],
        out_specs=[
            pl.BlockSpec((SNAP, PX * PZ), lambda i: (i, 0)),
            pl.BlockSpec((SNAP, SNAP), lambda i: (0, 0)),
        ],
        out_shape=[
            jax.ShapeDtypeStruct((count, PX * PZ), jnp.float32),
            jax.ShapeDtypeStruct((SNAP, SNAP), jnp.float32),
        ],
        scratch_shapes=[pltpu.VMEM((PX, SNAP, PZ), jnp.float32)],
    )(filter_taps, span, planes)


def basis_kernel(inv_ref, matrix_ref, basis_ref, gram_ref):
    @pl.when(pl.program_id(0) == 0)
    def _():
        gram_ref[...] = jnp.zeros(gram_ref.shape, jnp.float32)

    basis = jnp.dot(
        inv_ref[...],
        matrix_ref[...],
        precision=lax.Precision.HIGHEST,
        preferred_element_type=jnp.float32,
    )
    basis_ref[...] = basis
    gram_ref[...] += lax.dot_general(
        basis,
        basis,
        (((1,), (1,)), ((), ())),
        precision=lax.Precision.HIGHEST,
        preferred_element_type=jnp.float32,
    )


def basis_and_gram(inverse, matrix):
    count, width = matrix.shape
    size = inverse.shape[0]
    return pl.pallas_call(
        basis_kernel,
        grid=(count // size,),
        in_specs=[
            pl.BlockSpec((size, size), lambda i: (0, 0)),
            pl.BlockSpec((size, width), lambda i: (i, 0)),
        ],
        out_specs=[
            pl.BlockSpec((size, width), lambda i: (i, 0)),
            pl.BlockSpec((size, size), lambda i: (0, 0)),
        ],
        out_shape=[
            jax.ShapeDtypeStruct((count, width), jnp.float32),
            jax.ShapeDtypeStruct((size, size), jnp.float32),
        ],
    )(inverse, matrix)


def modes_kernel(inv_ref, basis_ref, modes_ref, *, scale):
    modes_ref[...] = (
        jnp.dot(
            inv_ref[...],
            basis_ref[...],
            precision=lax.Precision.HIGHEST,
            preferred_element_type=jnp.float32,
        )
        * scale
    )


def modes_of(inverse, basis, scale):
    count, width = basis.shape
    size = inverse.shape[0]
    return pl.pallas_call(
        functools.partial(modes_kernel, scale=scale),
        grid=(count // size,),
        in_specs=[
            pl.BlockSpec((size, size), lambda i: (0, 0)),
            pl.BlockSpec((size, width), lambda i: (i, 0)),
        ],
        out_specs=pl.BlockSpec((size, width), lambda i: (i, 0)),
        out_shape=jax.ShapeDtypeStruct((count, width), jnp.float32),
    )(inverse, basis)


def route_kernel(slot_ref, records_ref, buffer_ref, planes_ref):
    rows = buffer_ref.shape[0]
    first = pl.program_id(0) * rows
    places = first + lax.broadcasted_iota(jnp.int32, (rows, slot_ref.shape[1]), 0)
    pick = (slot_ref[...] == places).astype(jnp.bfloat16)
    for x in range(PX):
        planes_ref[x] = jnp.dot(
            pick, records_ref[:, x * PZ : (x + 1) * PZ], preferred_element_type=jnp.float32
        ).astype(jnp.bfloat16)
    buffer_ref[...] = pltpu.einshape("akb->kab", planes_ref[...])


def route_records(slot, records, slots, rows=512):
    count, width = records.shape
    return pl.pallas_call(
        route_kernel,
        grid=(slots // rows,),
        in_specs=[
            pl.BlockSpec((1, count), lambda i: (0, 0)),
            pl.BlockSpec((count, width), lambda i: (0, 0)),
        ],
        out_specs=pl.BlockSpec((rows, PX, PZ), lambda i: (i, 0, 0)),
        out_shape=jax.ShapeDtypeStruct((slots, PX, PZ), jnp.bfloat16),
        scratch_shapes=[pltpu.VMEM((PX, rows, PZ), jnp.bfloat16)],
    )(slot.reshape(1, count), records)


def swap_kernel(planes_ref, records_ref):
    records_ref[...] = pltpu.einshape("akb->kab", planes_ref[...])


def planes_to_records(planes, rows=256):
    width, count, lanes = planes.shape
    return pl.pallas_call(
        swap_kernel,
        grid=(count // rows,),
        in_specs=[pl.BlockSpec((width, rows, lanes), lambda i: (0, i, 0))],
        out_specs=pl.BlockSpec((rows, width, lanes), lambda i: (i, 0, 0)),
        out_shape=jax.ShapeDtypeStruct((count, width, lanes), planes.dtype),
    )(planes)


def doubling_inverse(lower):
    size = lower.shape[0]
    row = lax.broadcasted_iota(jnp.int32, lower.shape, 0)
    col = lax.broadcasted_iota(jnp.int32, lower.shape, 1)
    inverse = jnp.where(row == col, 1.0 / lower, 0.0)
    level = 0
    while (1 << level) < size:
        same_pair = lax.shift_right_logical(row, level + 1) == lax.shift_right_logical(col, level + 1)
        other_half = lax.shift_right_logical(row, level) != lax.shift_right_logical(col, level)
        coupling = jnp.where(same_pair & other_half, lower, 0.0)
        step = jnp.dot(
            inverse, coupling, precision=lax.Precision.HIGHEST, preferred_element_type=jnp.float32
        )
        inverse = inverse - jnp.dot(
            step, inverse, precision=lax.Precision.HIGHEST, preferred_element_type=jnp.float32
        )
        level += 1
    return inverse


def nt_dot(a, b):
    return lax.dot_general(
        a, b, (((1,), (1,)), ((), ())), precision=lax.Precision.HIGHEST,
        preferred_element_type=jnp.float32,
    )


def nn_dot(a, b):
    return jnp.dot(a, b, precision=lax.Precision.HIGHEST, preferred_element_type=jnp.float32)


def first_half_kernel(lower_a_ref, gram_ref, inv_a_ref, lower_b_ref, rest_ref):
    half = lower_a_ref.shape[0]
    inv_a = doubling_inverse(lower_a_ref[...])
    inv_a_ref[...] = inv_a
    lower_b = nt_dot(gram_ref[half:, :half], inv_a)
    lower_b_ref[...] = lower_b
    rest_ref[...] = gram_ref[half:, half:] - nt_dot(lower_b, lower_b)


def second_half_kernel(lower_a_ref, lower_b_ref, lower_c_ref, inv_a_ref, lower_ref, inverse_ref):
    half = lower_a_ref.shape[0]
    inv_c = doubling_inverse(lower_c_ref[...])
    inv_a = inv_a_ref[...]
    zero = jnp.zeros((half, half), jnp.float32)
    lower_ref[:half, :half] = lower_a_ref[...]
    lower_ref[:half, half:] = zero
    lower_ref[half:, :half] = lower_b_ref[...]
    lower_ref[half:, half:] = lower_c_ref[...]
    inverse_ref[:half, :half] = inv_a
    inverse_ref[:half, half:] = zero
    inverse_ref[half:, :half] = -nn_dot(inv_c, nn_dot(lower_b_ref[...], inv_a))
    inverse_ref[half:, half:] = inv_c


def last_half_kernel(
    lower_a_ref, lower_b_ref, lower_c_ref, inv_a_ref, first_ref, lower_ref, inverse_ref, r_ref, *, scale
):
    second_half_kernel(lower_a_ref, lower_b_ref, lower_c_ref, inv_a_ref, lower_ref, inverse_ref)
    r_ref[...] = jnp.transpose(nn_dot(first_ref[...], lower_ref[...])) / scale


def gram_of(matrix):
    return lax.dot_general(
        matrix,
        matrix,
        (((1,), (1,)), ((), ())),
        precision=lax.Precision.HIGHEST,
        preferred_element_type=jnp.float32,
    )


def high_dot(a, b, dims):
    return lax.dot_general(
        a, b, (dims, ((), ())), precision=lax.Precision.HIGHEST, preferred_element_type=jnp.float32
    )


def factor_and_inverse(gram, first=None, scale=1.0):
    size = gram.shape[0]
    half = size // 2
    gram = (gram + gram.T) / 2
    lower_a = lax.linalg.cholesky(gram[:half, :half], symmetrize_input=False)
    square = jax.ShapeDtypeStruct((half, half), jnp.float32)
    inv_a, lower_b, rest = pl.pallas_call(
        first_half_kernel, out_shape=[square, square, square]
    )(lower_a, gram)
    lower_c = lax.linalg.cholesky(rest, symmetrize_input=False)
    full = jax.ShapeDtypeStruct((size, size), jnp.float32)
    if first is None:
        return pl.pallas_call(second_half_kernel, out_shape=[full, full])(
            lower_a, lower_b, lower_c, inv_a
        )
    return pl.pallas_call(
        functools.partial(last_half_kernel, scale=scale), out_shape=[full, full, full]
    )(lower_a, lower_b, lower_c, inv_a, first)


def sum_over_devices(part, axes, devices_all):
    rows = part.reshape(devices_all, -1)
    rows = lax.all_to_all(rows, axes, 0, 0, tiled=True)
    total = jnp.sum(rows, axis=0, keepdims=True)
    total = jnp.broadcast_to(total, rows.shape)
    total = lax.all_to_all(total, axes, 0, 0, tiled=True)
    return total.reshape(part.shape)


def local(records, record_owner, record_field, filter_taps):
    devices_all = lax.axis_size(("gx", "gy"))
    rec_count = records.shape[0]
    cells = records.shape[1]
    capacity = 2 * (rec_count // devices_all)
    onehot = (record_owner[:, None] == jnp.arange(devices_all, dtype=jnp.int32)[None, :]).astype(
        jnp.int32
    )
    position = jnp.sum((jnp.cumsum(onehot, axis=0) - 1) * onehot, axis=1)
    slot = record_owner * capacity + position
    places = jnp.arange(devices_all * capacity, dtype=jnp.int32)
    pick = slot[None, :] == places[:, None]
    buffer = route_records(slot, records, devices_all * capacity)
    labels = jnp.sum(jnp.where(pick, record_field[None, :] + 1, 0), axis=1) - 1
    arrived, arrived_labels = (
        lax.all_to_all(
            buffer.reshape(devices_all, capacity, PX, PZ),
            ("gx", "gy"),
            split_axis=0,
            concat_axis=0,
            tiled=True,
        ),
        lax.all_to_all(
            labels.reshape(devices_all, capacity),
            ("gx", "gy"),
            split_axis=0,
            concat_axis=0,
            tiled=True,
        ),
    )
    flat_data = arrived.reshape(devices_all * capacity, PX, PZ)
    flat_labels = arrived_labels.reshape(devices_all * capacity)
    target = (flat_labels % 3) * SNAP + flat_labels // 3
    target = jnp.where(flat_labels >= 0, target, -1)
    order = target[None, :] == jnp.arange(rec_count, dtype=jnp.int32)[:, None]
    planes = jnp.einsum(
        "tk,kab->atb", order.astype(jnp.bfloat16), flat_data, preferred_element_type=jnp.float32
    ).astype(jnp.bfloat16)
    fields, gram_one = filter_planes(planes, filter_taps)
    lower_one, inv_one = factor_and_inverse(sum_over_devices(gram_one, ("gx", "gy"), devices_all))
    basis_one, gram_two = basis_and_gram(inv_one, fields)
    scale = math.sqrt(3.0 * cells * devices_all)
    lower_two, inv_two, r_factor = factor_and_inverse(
        sum_over_devices(gram_two, ("gx", "gy"), devices_all), lower_one, scale
    )
    modes = modes_of(inv_two, basis_one, scale).reshape(3, SNAP, cells)
    first_factor = lower_one.T / scale
    return (modes.transpose(1, 0, 2), r_factor, first_factor)


def solution(mesh):
    placed = (P(("gx", "gy"), None), P(("gx", "gy")), P(("gx", "gy")), P())
    return jax.shard_map(
        local,
        mesh=mesh,
        in_specs=placed,
        out_specs=(P(None, None, ("gx", "gy")), P(), P()),
        check_vma=False,
    )
```

```python
import functools
import math

import jax
import jax.numpy as jnp
from jax import lax
from jax.experimental import pallas as pl
from jax.experimental.pallas import tpu as pltpu
from jax.sharding import PartitionSpec as P

SNAP = 256
PX = 16
PZ = 128


def circulant(tap_row, period):
    places = jnp.arange(period, dtype=jnp.int32)
    offsets = jnp.arange(9, dtype=jnp.int32) - 4
    target = (places[None, :, None] + offsets[:, None, None]) % period
    onehot = (target == places[None, None, :]).astype(jnp.float32)
    return jnp.einsum("k,kxa->xa", tap_row, onehot, precision=lax.Precision.HIGHEST)


def split_three(matrix):
    high = lax.reduce_precision(matrix, exponent_bits=8, mantissa_bits=7)
    rest = matrix - high
    mid = lax.reduce_precision(rest, exponent_bits=8, mantissa_bits=7)
    low = rest - mid
    return jnp.concatenate([high, mid, low], axis=1).astype(jnp.bfloat16)


def filter_kernel(taps_ref, span_ref, planes_ref, out_ref, gram_ref, spread_ref):
    taps = taps_ref.shape[1]
    reach = (taps - 1) // 2
    span = span_ref[...]

    @pl.when(pl.program_id(0) == 0)
    def _():
        gram_ref[...] = jnp.zeros(gram_ref.shape, jnp.float32)

    for x in range(PX):
        parts = jnp.dot(planes_ref[x], span, preferred_element_type=jnp.float32)
        spread_ref[x] = parts[:, :PZ] + parts[:, PZ : 2 * PZ] + parts[:, 2 * PZ :]
    for x in range(PX):
        acc = taps_ref[0, 0] * spread_ref[(x - reach) % PX]
        for k in range(1, taps):
            acc = acc + taps_ref[0, k] * spread_ref[(x + k - reach) % PX]
        out_ref[:, x * PZ : (x + 1) * PZ] = acc
    block = out_ref[...]
    gram_ref[...] += lax.dot_general(
        block,
        block,
        (((1,), (1,)), ((), ())),
        precision=lax.Precision.HIGHEST,
        preferred_element_type=jnp.float32,
    )


def filter_planes(planes, filter_taps):
    count = planes.shape[1]
    span = split_three(circulant(filter_taps[1], PZ).T)
    return pl.pallas_call(
        filter_kernel,
        grid=(count // SNAP,),
        in_specs=[
            pl.BlockSpec(memory_space=pltpu.SMEM),
            pl.BlockSpec((PZ, 3 * PZ), lambda i: (0, 0)),
            pl.BlockSpec((PX, SNAP, PZ), lambda i: (0, i, 0)),
        ],
        out_specs=[
            pl.BlockSpec((SNAP, PX * PZ), lambda i: (i, 0)),
            pl.BlockSpec((SNAP, SNAP), lambda i: (0, 0)),
        ],
        out_shape=[
            jax.ShapeDtypeStruct((count, PX * PZ), jnp.float32),
            jax.ShapeDtypeStruct((SNAP, SNAP), jnp.float32),
        ],
        scratch_shapes=[pltpu.VMEM((PX, SNAP, PZ), jnp.float32)],
    )(filter_taps, span, planes)


def basis_kernel(inv_ref, matrix_ref, basis_ref, gram_ref):
    @pl.when(pl.program_id(0) == 0)
    def _():
        gram_ref[...] = jnp.zeros(gram_ref.shape, jnp.float32)

    basis = jnp.dot(
        inv_ref[...],
        matrix_ref[...],
        precision=lax.Precision.HIGHEST,
        preferred_element_type=jnp.float32,
    )
    basis_ref[...] = basis
    gram_ref[...] += lax.dot_general(
        basis,
        basis,
        (((1,), (1,)), ((), ())),
        precision=lax.Precision.HIGHEST,
        preferred_element_type=jnp.float32,
    )


def basis_and_gram(inverse, matrix):
    count, width = matrix.shape
    size = inverse.shape[0]
    return pl.pallas_call(
        basis_kernel,
        grid=(count // size,),
        in_specs=[
            pl.BlockSpec((size, size), lambda i: (0, 0)),
            pl.BlockSpec((size, width), lambda i: (i, 0)),
        ],
        out_specs=[
            pl.BlockSpec((size, width), lambda i: (i, 0)),
            pl.BlockSpec((size, size), lambda i: (0, 0)),
        ],
        out_shape=[
            jax.ShapeDtypeStruct((count, width), jnp.float32),
            jax.ShapeDtypeStruct((size, size), jnp.float32),
        ],
    )(inverse, matrix)


def modes_kernel(inv_ref, basis_ref, modes_ref, *, scale):
    modes_ref[...] = (
        jnp.dot(
            inv_ref[...],
            basis_ref[...],
            precision=lax.Precision.HIGHEST,
            preferred_element_type=jnp.float32,
        )
        * scale
    )


def modes_of(inverse, basis, scale):
    count, width = basis.shape
    size = inverse.shape[0]
    return pl.pallas_call(
        functools.partial(modes_kernel, scale=scale),
        grid=(count // size,),
        in_specs=[
            pl.BlockSpec((size, size), lambda i: (0, 0)),
            pl.BlockSpec((size, width), lambda i: (i, 0)),
        ],
        out_specs=pl.BlockSpec((size, width), lambda i: (i, 0)),
        out_shape=jax.ShapeDtypeStruct((count, width), jnp.float32),
    )(inverse, basis)


def route_kernel(slot_ref, records_ref, buffer_ref, planes_ref):
    rows = buffer_ref.shape[0]
    first = pl.program_id(0) * rows
    places = first + lax.broadcasted_iota(jnp.int32, (rows, slot_ref.shape[1]), 0)
    pick = (slot_ref[...] == places).astype(jnp.bfloat16)
    for x in range(PX):
        planes_ref[x] = jnp.dot(
            pick, records_ref[:, x * PZ : (x + 1) * PZ], preferred_element_type=jnp.float32
        ).astype(jnp.bfloat16)
    buffer_ref[...] = pltpu.einshape("akb->kab", planes_ref[...])


def route_records(slot, records, slots, rows=512):
    count, width = records.shape
    return pl.pallas_call(
        route_kernel,
        grid=(slots // rows,),
        in_specs=[
            pl.BlockSpec((1, count), lambda i: (0, 0)),
            pl.BlockSpec((count, width), lambda i: (0, 0)),
        ],
        out_specs=pl.BlockSpec((rows, PX, PZ), lambda i: (i, 0, 0)),
        out_shape=jax.ShapeDtypeStruct((slots, PX, PZ), jnp.bfloat16),
        scratch_shapes=[pltpu.VMEM((PX, rows, PZ), jnp.bfloat16)],
    )(slot.reshape(1, count), records)


def swap_kernel(planes_ref, records_ref):
    records_ref[...] = pltpu.einshape("akb->kab", planes_ref[...])


def planes_to_records(planes, rows=256):
    width, count, lanes = planes.shape
    return pl.pallas_call(
        swap_kernel,
        grid=(count // rows,),
        in_specs=[pl.BlockSpec((width, rows, lanes), lambda i: (0, i, 0))],
        out_specs=pl.BlockSpec((rows, width, lanes), lambda i: (i, 0, 0)),
        out_shape=jax.ShapeDtypeStruct((count, width, lanes), planes.dtype),
    )(planes)


def doubling_inverse(lower):
    size = lower.shape[0]
    row = lax.broadcasted_iota(jnp.int32, lower.shape, 0)
    col = lax.broadcasted_iota(jnp.int32, lower.shape, 1)
    inverse = jnp.where(row == col, 1.0 / lower, 0.0)
    level = 0
    while (1 << level) < size:
        same_pair = lax.shift_right_logical(row, level + 1) == lax.shift_right_logical(col, level + 1)
        other_half = lax.shift_right_logical(row, level) != lax.shift_right_logical(col, level)
        coupling = jnp.where(same_pair & other_half, lower, 0.0)
        step = jnp.dot(
            inverse, coupling, precision=lax.Precision.HIGHEST, preferred_element_type=jnp.float32
        )
        inverse = inverse - jnp.dot(
            step, inverse, precision=lax.Precision.HIGHEST, preferred_element_type=jnp.float32
        )
        level += 1
    return inverse


def nt_dot(a, b):
    return lax.dot_general(
        a, b, (((1,), (1,)), ((), ())), precision=lax.Precision.HIGHEST,
        preferred_element_type=jnp.float32,
    )


def nn_dot(a, b):
    return jnp.dot(a, b, precision=lax.Precision.HIGHEST, preferred_element_type=jnp.float32)


def first_half_kernel(lower_a_ref, gram_ref, inv_a_ref, lower_b_ref, rest_ref):
    half = lower_a_ref.shape[0]
    inv_a = doubling_inverse(lower_a_ref[...])
    inv_a_ref[...] = inv_a
    lower_b = nt_dot(gram_ref[half:, :half], inv_a)
    lower_b_ref[...] = lower_b
    far = gram_ref[half:, half:]
    rest_ref[...] = (far + far.T) / 2 - nt_dot(lower_b, lower_b)


def second_half_kernel(lower_a_ref, lower_b_ref, lower_c_ref, inv_a_ref, lower_ref, inverse_ref):
    half = lower_a_ref.shape[0]
    inv_c = doubling_inverse(lower_c_ref[...])
    inv_a = inv_a_ref[...]
    zero = jnp.zeros((half, half), jnp.float32)
    lower_ref[:half, :half] = lower_a_ref[...]
    lower_ref[:half, half:] = zero
    lower_ref[half:, :half] = lower_b_ref[...]
    lower_ref[half:, half:] = lower_c_ref[...]
    inverse_ref[:half, :half] = inv_a
    inverse_ref[:half, half:] = zero
    inverse_ref[half:, :half] = -nn_dot(inv_c, nn_dot(lower_b_ref[...], inv_a))
    inverse_ref[half:, half:] = inv_c


def last_half_kernel(
    lower_a_ref, lower_b_ref, lower_c_ref, inv_a_ref, first_ref, lower_ref, inverse_ref, r_ref, *, scale
):
    second_half_kernel(lower_a_ref, lower_b_ref, lower_c_ref, inv_a_ref, lower_ref, inverse_ref)
    r_ref[...] = jnp.transpose(nn_dot(first_ref[...], lower_ref[...])) / scale


def gram_of(matrix):
    return lax.dot_general(
        matrix,
        matrix,
        (((1,), (1,)), ((), ())),
        precision=lax.Precision.HIGHEST,
        preferred_element_type=jnp.float32,
    )


def high_dot(a, b, dims):
    return lax.dot_general(
        a, b, (dims, ((), ())), precision=lax.Precision.HIGHEST, preferred_element_type=jnp.float32
    )


def factor_and_inverse(gram, first=None, scale=1.0):
    size = gram.shape[0]
    half = size // 2
    corner = gram[:half, :half]
    lower_a = lax.linalg.cholesky((corner + corner.T) / 2, symmetrize_input=False)
    square = jax.ShapeDtypeStruct((half, half), jnp.float32)
    inv_a, lower_b, rest = pl.pallas_call(
        first_half_kernel, out_shape=[square, square, square]
    )(lower_a, gram)
    lower_c = lax.linalg.cholesky(rest, symmetrize_input=False)
    full = jax.ShapeDtypeStruct((size, size), jnp.float32)
    if first is None:
        return pl.pallas_call(second_half_kernel, out_shape=[full, full])(
            lower_a, lower_b, lower_c, inv_a
        )
    return pl.pallas_call(
        functools.partial(last_half_kernel, scale=scale), out_shape=[full, full, full]
    )(lower_a, lower_b, lower_c, inv_a, first)


def sum_over_devices(part, axes, devices_all):
    rows = part.reshape(devices_all, -1)
    rows = lax.all_to_all(rows, axes, 0, 0, tiled=True)
    total = jnp.sum(rows, axis=0, keepdims=True)
    total = jnp.broadcast_to(total, rows.shape)
    total = lax.all_to_all(total, axes, 0, 0, tiled=True)
    return total.reshape(part.shape)


def local(records, record_owner, record_field, filter_taps):
    devices_all = lax.axis_size(("gx", "gy"))
    rec_count = records.shape[0]
    cells = records.shape[1]
    capacity = 2 * (rec_count // devices_all)
    onehot = (record_owner[:, None] == jnp.arange(devices_all, dtype=jnp.int32)[None, :]).astype(
        jnp.int32
    )
    position = jnp.sum((jnp.cumsum(onehot, axis=0) - 1) * onehot, axis=1)
    slot = record_owner * capacity + position
    places = jnp.arange(devices_all * capacity, dtype=jnp.int32)
    pick = slot[None, :] == places[:, None]
    buffer = route_records(slot, records, devices_all * capacity)
    labels = jnp.sum(jnp.where(pick, record_field[None, :] + 1, 0), axis=1) - 1
    arrived, arrived_labels = (
        lax.all_to_all(
            buffer.reshape(devices_all, capacity, PX, PZ),
            ("gx", "gy"),
            split_axis=0,
            concat_axis=0,
            tiled=True,
        ),
        lax.all_to_all(
            labels.reshape(devices_all, capacity),
            ("gx", "gy"),
            split_axis=0,
            concat_axis=0,
            tiled=True,
        ),
    )
    flat_data = arrived.reshape(devices_all * capacity, PX, PZ)
    flat_labels = arrived_labels.reshape(devices_all * capacity)
    target = (flat_labels % 3) * SNAP + flat_labels // 3
    target = jnp.where(flat_labels >= 0, target, -1)
    order = target[None, :] == jnp.arange(rec_count, dtype=jnp.int32)[:, None]
    planes = jnp.einsum(
        "tk,kab->atb", order.astype(jnp.bfloat16), flat_data, preferred_element_type=jnp.float32
    ).astype(jnp.bfloat16)
    fields, gram_one = filter_planes(planes, filter_taps)
    lower_one, inv_one = factor_and_inverse(sum_over_devices(gram_one, ("gx", "gy"), devices_all))
    basis_one, gram_two = basis_and_gram(inv_one, fields)
    scale = math.sqrt(3.0 * cells * devices_all)
    lower_two, inv_two, r_factor = factor_and_inverse(
        sum_over_devices(gram_two, ("gx", "gy"), devices_all), lower_one, scale
    )
    modes = modes_of(inv_two, basis_one, scale).reshape(3, SNAP, cells)
    first_factor = lower_one.T / scale
    return (modes.transpose(1, 0, 2), r_factor, first_factor)


def solution(mesh):
    placed = (P(("gx", "gy"), None), P(("gx", "gy")), P(("gx", "gy")), P())
    return jax.shard_map(
        local,
        mesh=mesh,
        in_specs=placed,
        out_specs=(P(None, None, ("gx", "gy")), P(), P()),
        check_vma=False,
    )
```
